32 devices in a mesh: ctx: 4 (over y, core), ep: 8 (over z, x).
Axes of the slice: x: 2, y: 2, z: 4, core: 2. Of those that a mesh axis runs over, the one named last changes fastest.
Arguments:
- hidden_state: bfloat16 [512, 2048], P(('ctx', 'ep')), may hold values from -200 to 200
- upstream_grad: bfloat16 [512, 2048], P(('ctx', 'ep')), may hold values from -6 to 6
- route_ids: int32 [512, 6], P(('ctx', 'ep')), may hold values from 0 to 31, all different within a row; in each aligned block of 16 rows (0 to 15, 16 to 31, ...) at most 6 rows name the same one
- route_gates: float32 [512, 6], P(('ctx', 'ep')), may hold values from 0.05 to 0.5
- norm_gain: float32 [2048], replicated, may hold values from 0.25 to 1.75
- w_gate: bfloat16 [8, 4, 1408, 2048], P('ep', 'ctx'), may hold values from -0.125 to 0.125
- w_up: bfloat16 [8, 4, 1408, 2048], P('ep', 'ctx'), may hold values from -0.125 to 0.125
- w_down: bfloat16 [8, 4, 1408, 2048], P('ep', 'ctx'), may hold values from -0.15625 to 0.15625
- out_proj: bfloat16 [2048, 2048], P('ep'), may hold values from -0.125 to 0.125
- queries: bfloat16 [512, 2048], P('ctx', 'ep'), may hold values from -12 to 12
- key_rows: bfloat16 [512, 2048], P('ctx', 'ep'), may hold values from -12 to 12
- value_rows: bfloat16 [512, 2048], P('ctx', 'ep'), may hold values from -6 to 6
Outputs:
- grad_state: bfloat16 [512, 2048], P(('ctx', 'ep'))
- grad_queries: bfloat16 [512, 2048], P('ctx', 'ep')
- grad_keys: bfloat16 [512, 2048], P('ctx', 'ep')
- grad_values: bfloat16 [512, 2048], P('ctx', 'ep')
- grad_gate: bfloat16 [8, 4, 1408, 2048], P('ep', 'ctx')
- grad_up: bfloat16 [8, 4, 1408, 2048], P('ep', 'ctx')
- grad_down: bfloat16 [8, 4, 1408, 2048], P('ep', 'ctx')
The draws below stay inside these ranges and needn't reach their ends.
Inputs may be any that keep to these rules, and one draw needn't show every extreme that they name: `route_ids`: within the 16 tokens of one routing block no expert is named by more than 6 routes, a bound that some block reaches.
All inputs are finite; a program needn't handle non-finite values.
Results may differ from the reference program's by a relative error of at most 0.015.
Values may be sent and summed in bfloat16 or wider, within the bound.
No kernel may reach another device: no remote copies, remote signals or barrier semaphores. Data moves between devices by JAX's collectives and lax.ppermute only.
A program may use at most 128 MiB of HBM per device.

```python
import math
import jax
import jax.numpy as jnp
import numpy as np
from jax import lax

D = 2048
HEADS = 16
HD = 128
FF = 1408
TOPK = 6
EXP_DEV = 4
EXPERTS = 32
SEQ = 512
TOK_DEV = 16
HID_DEV = 1408
CAP = 6
N_CTX = 4
N_EP = 8


def draw_hidden_state(key, part):
    base = jax.random.normal(jax.random.fold_in(key, 1), (SEQ, D), jnp.float32)
    row_scale = jnp.exp(jax.random.uniform(jax.random.fold_in(key, 2), (SEQ, 1), jnp.float32) * math.log(10.0))
    column_scale = jnp.exp(jax.random.uniform(jax.random.fold_in(key, 3), (1, D), jnp.float32) * math.log(10.0))
    return (jnp.clip(base, -6.0, 6.0) * row_scale * column_scale * 0.3).astype(jnp.bfloat16)


def drawn_pair(key):
    columns = HEADS * HD
    query_draw = jnp.clip(jax.random.normal(jax.random.fold_in(key, 11), (SEQ, columns), jnp.float32), -6.0, 6.0)
    key_draw = jnp.clip(jax.random.normal(jax.random.fold_in(key, 12), (SEQ, columns), jnp.float32), -6.0, 6.0)
    return (query_draw, key_draw)


def draw_queries(key, part):
    return drawn_pair(key)[0].astype(jnp.bfloat16)


def draw_key_rows(key, part):
    return drawn_pair(key)[1].astype(jnp.bfloat16)


def block_levels(own_key, extent, cuts, low, largest):
    loudness, own = 1.0, jax.random.fold_in(own_key, 6)
    for position, shards_of in cuts:
        draws = jnp.exp(jax.random.uniform(jax.random.fold_in(own, position), (shards_of,), jnp.float32, low / len(cuts), largest / len(cuts)))
        loudness = loudness * jnp.repeat(draws, extent[position] // shards_of).reshape([-1 if axis == position else 1 for axis in range(len(extent))])
    return loudness


def routed_block(key, own, number, rows, amount, top, most, lean):
    ranking = jax.random.permutation(key, amount)
    packed, common = load_shares(amount, rows * top, most, lean, True), load_shares(amount, rows * top, most, lean, False)
    places = jnp.arange(amount)

    def named(tallies, rotation):
        used = int((tallies > 0).sum())
        fixed = max(1, used // 4)
        shifted = fixed + (places - fixed + rotation * (used - fixed)) % max(1, amount - fixed)
        return jnp.zeros((amount,), jnp.int32).at[ranking[jnp.where(places < fixed, places, shifted)]].set(jnp.asarray(tallies, jnp.int32))

    tallies = jnp.where(number % 4 == 0, named(packed, number // 4), named(common, number - number // 4 - 1))
    mixed = jax.random.permutation(jax.random.fold_in(own, 3), amount)
    donor, receiver = mixed[0:amount // 2 * 2:2], mixed[1:amount // 2 * 2:2]
    margin = jnp.minimum(tallies[donor] - 1, most - tallies[receiver]) // 2
    margin = jnp.where((donor == ranking[0]) | (receiver == ranking[0]) | (tallies[receiver] == 0), 0, jnp.maximum(margin, 0))
    shifted = jax.random.randint(jax.random.fold_in(own, 4), (amount // 2,), 0, 1 << 20) % (margin + 1)
    tallies = tallies.at[donor].add(-shifted).at[receiver].add(shifted)
    labels = jnp.searchsorted(jnp.cumsum(tallies), jnp.arange(rows * top), side="right").astype(jnp.int32)
    listing = labels.reshape(top, rows).T
    listing = listing[jax.random.permutation(jax.random.fold_in(own, 1), rows)]
    rotation = jax.random.randint(jax.random.fold_in(own, 2), (rows, 1), 0, top)
    return jnp.take_along_axis(listing, (jnp.arange(top)[None, :] + rotation) % top, axis=1)


def load_shares(number_of, total, bound, lean, full):
    weights = [(1 << 20) // math.isqrt(standing ** lean) + 1 for standing in range(1, number_of + 1)]
    largest = bound if full else min(bound, max(-(-total // number_of), total * weights[0] // sum(weights)))
    least = 1 if total - largest >= number_of - 1 else 0
    holding, surplus = [largest] + [least] * (number_of - 1), total - largest - least * (number_of - 1)
    while surplus > 0:
        movable = [i for i in range(1, number_of) if holding[i] < largest] or [i for i in range(1, number_of) if holding[i] < bound]
        whole, remaining = sum([weights[i] for i in movable]), surplus
        for i in movable:
            more = min(bound - holding[i], max(1, remaining * weights[i] // whole), surplus)
            holding[i] = holding[i] + more
            surplus = surplus - more
    return np.array(holding)


def centred(own_key, extent, width, bound, shards=(), held_as=jnp.bfloat16):
    drawn = jax.random.normal(own_key, extent, jnp.float32) * width
    if len(shards) > 0:
        drawn = block_levels(own_key, extent, shards, -0.22, 0.18) * drawn
    return jnp.clip(drawn, min=-bound, max=bound).astype(held_as)


def setup_inputs(seed: int = 0) -> dict:
    seeds = jax.random.split(jax.random.key(seed), 13)
    hidden_state = draw_hidden_state(jax.random.fold_in(seeds[12], 71), 0)
    upstream_grad = centred(seeds[1], (SEQ, D), 1.0, 6.0, ((0, 32),))
    route_ids_keys = jax.random.split(jax.random.fold_in(seeds[2], 1), SEQ // TOK_DEV)
    route_ids_turns = jax.random.permutation(jax.random.fold_in(seeds[2], 3), SEQ // TOK_DEV)
    route_ids = jax.vmap(lambda own, number: routed_block(jax.random.fold_in(seeds[2], 2), own, number, TOK_DEV, EXPERTS, TOPK, CAP, 2))(route_ids_keys, route_ids_turns).reshape((SEQ, TOPK))
    route_gates = jnp.clip(jnp.exp(math.log(0.5) - 2.3025851 * jax.random.uniform(seeds[3], (SEQ, TOPK), jnp.float32) ** block_levels(seeds[3], (SEQ, TOPK), ((0, 32),), -0.2, 0.2)), 0.05, 0.5)
    norm_gain = jnp.clip(1.0 + 0.15 * jax.random.normal(seeds[4], (D,), jnp.float32), 0.25, 1.75)
    w_gate = centred(seeds[5], (N_EP, N_CTX, HID_DEV, D), D ** -0.5, 0.125, ((0, 8), (1, 4)))
    w_up = centred(seeds[6], (N_EP, N_CTX, HID_DEV, D), D ** -0.5, 0.125, ((0, 8), (1, 4)))
    w_down = centred(seeds[7], (N_EP, N_CTX, HID_DEV, D), FF ** -0.5, 0.15625, ((0, 8), (1, 4)))
    out_proj = centred(seeds[8], (HEADS * HD, D), D ** -0.5, 0.125, ((0, 8),))
    queries = draw_queries(jax.random.fold_in(seeds[12], 71), 0)
    key_rows = draw_key_rows(jax.random.fold_in(seeds[12], 71), 0)
    value_rows = centred(seeds[11], (SEQ, HEADS * HD), 1.0, 6.0, ((0, 4), (1, 8)))
    return {"hidden_state": hidden_state, "upstream_grad": upstream_grad, "route_ids": route_ids, "route_gates": route_gates, "norm_gain": norm_gain, "w_gate": w_gate, "w_up": w_up, "w_down": w_down, "out_proj": out_proj, "queries": queries, "key_rows": key_rows, "value_rows": value_rows}


EPSILON = 1e-06
FLOOR_SCORE = -1e+30
PRECISE = lax.Precision.HIGHEST

def expert_pass(token_rows, grad_rows, gate_rows, up_rows, down_rows):
    contract = (((1,), (1,)), ((), ()))
    over_rows = (((0,), (0,)), ((), ()))
    pre_gate = lax.dot_general(token_rows, gate_rows, contract, preferred_element_type=jnp.float32)
    up_value = lax.dot_general(token_rows, up_rows, contract, preferred_element_type=jnp.float32)
    sigmoid = jax.nn.sigmoid(pre_gate)
    activation = (pre_gate * sigmoid * up_value).astype(jnp.bfloat16)
    act_grad = lax.dot_general(grad_rows, down_rows, contract, preferred_element_type=jnp.float32)
    up_grad = (act_grad * pre_gate * sigmoid).astype(jnp.bfloat16)
    gate_grad = (act_grad * up_value * sigmoid * (1.0 + pre_gate * (1.0 - sigmoid))).astype(jnp.bfloat16)
    partial_value = (jnp.dot(gate_grad, gate_rows, preferred_element_type=jnp.float32) + jnp.dot(up_grad, up_rows, preferred_element_type=jnp.float32)).astype(jnp.bfloat16)
    gate_total = lax.dot_general(gate_grad, token_rows, over_rows, preferred_element_type=jnp.float32)
    up_total = lax.dot_general(up_grad, token_rows, over_rows, preferred_element_type=jnp.float32)
    down_total = lax.dot_general(activation, grad_rows, over_rows, preferred_element_type=jnp.float32)
    return (partial_value, gate_total, up_total, down_total)

def head_grads(operands):
    query_head, key_head, value_head, dout_head = operands
    scale = 1.0 / math.sqrt(HD)
    positions = jnp.arange(SEQ, dtype=jnp.int32)
    allowed = positions[:, None] >= positions[None, :]
    raw_scores = jnp.dot(query_head, key_head.T, preferred_element_type=jnp.float32) * scale
    row_top = lax.optimization_barrier(jnp.max(jnp.where(allowed, raw_scores, FLOOR_SCORE), axis=1, keepdims=True))
    row_total = lax.optimization_barrier(jnp.sum(jnp.where(allowed, jnp.exp(raw_scores - row_top), 0.0), axis=1, keepdims=True))
    log_total = row_top + jnp.log(row_total)
    probs = jnp.where(allowed, jnp.exp(raw_scores - log_total), 0.0)
    attn_out = jnp.dot(probs, value_head.astype(jnp.float32), precision=PRECISE)
    row_delta = lax.optimization_barrier(jnp.sum(dout_head.astype(jnp.float32) * attn_out, axis=1, keepdims=True))
    grad_value = jnp.dot(probs.astype(jnp.bfloat16).T, dout_head, preferred_element_type=jnp.float32)
    prob_grad = jnp.dot(dout_head, value_head.T, preferred_element_type=jnp.float32)
    score_grad = (probs * (prob_grad - row_delta)).astype(jnp.bfloat16)
    grad_query = jnp.dot(score_grad, key_head, preferred_element_type=jnp.float32) * scale
    grad_key = jnp.dot(score_grad.T, query_head, preferred_element_type=jnp.float32) * scale
    return (grad_query.astype(jnp.bfloat16), grad_key.astype(jnp.bfloat16), grad_value.astype(jnp.bfloat16))

def reference(hidden_state, upstream_grad, route_ids, route_gates, norm_gain, w_gate, w_up, w_down, out_proj, queries, key_rows, value_rows):
    state = hidden_state.astype(jnp.float32)
    inv_rms = lax.rsqrt(lax.optimization_barrier(jnp.mean(state * state, axis=1, keepdims=True)) + EPSILON)
    normed = (state * inv_rms * norm_gain[None, :]).astype(jnp.bfloat16)
    route_count = TOK_DEV * TOPK
    block_count = SEQ // TOK_DEV
    flat_ids = route_ids.reshape(block_count, route_count)
    upstream_rep = jnp.repeat(upstream_grad, TOPK, axis=0).astype(jnp.float32).reshape(block_count, route_count, D)
    scaled_grads = (route_gates.reshape(block_count, route_count, 1) * upstream_rep).astype(jnp.bfloat16)
    normed_rep = jnp.repeat(normed, TOPK, axis=0).reshape(block_count, route_count, D).astype(jnp.float32)
    scaled_wide = scaled_grads.astype(jnp.float32)
    expert_ids = jnp.arange(EXPERTS, dtype=jnp.int32)
    matches = (flat_ids[:, :, None] == expert_ids[None, None, :]).astype(jnp.int32)
    earlier = jnp.cumsum(matches, axis=1) - matches
    slot_index = lax.optimization_barrier(jnp.sum(earlier * matches, axis=2))
    slot_ids = jnp.arange(CAP, dtype=jnp.int32)
    copies = N_CTX // EXP_DEV

    def one_expert(running, inputs):
        expert_id, gate_w, up_w, down_w = inputs
        dispatch = ((flat_ids == expert_id)[:, None, :] & (slot_index[:, None, :] == slot_ids[None, :, None])).astype(jnp.float32)
        token_rows = jnp.einsum('bcr,brd->bcd', dispatch, normed_rep, precision=PRECISE).astype(jnp.bfloat16).reshape(block_count * CAP, D)
        grad_rows = jnp.einsum('bcr,brd->bcd', dispatch, scaled_wide, precision=PRECISE).astype(jnp.bfloat16).reshape(block_count * CAP, D)
        summed = jnp.zeros((block_count * CAP, D), jnp.float32)
        gate_list, up_list, down_list = ([], [], [])
        for slice_index in range(copies):
            first_unit = slice_index * HID_DEV
            partial_value, gate_total, up_total, down_total = expert_pass(token_rows, grad_rows, gate_w[first_unit:first_unit + HID_DEV], up_w[first_unit:first_unit + HID_DEV], down_w[first_unit:first_unit + HID_DEV])
            summed = summed + partial_value.astype(jnp.float32)
            gate_list.append(gate_total.astype(jnp.bfloat16))
            up_list.append(up_total.astype(jnp.bfloat16))
            down_list.append(down_total.astype(jnp.bfloat16))
        returned = jnp.einsum('bcr,bcd->brd', dispatch, summed.reshape(block_count, CAP, D), precision=PRECISE)
        return (running + returned, (jnp.concatenate(gate_list, axis=0), jnp.concatenate(up_list, axis=0), jnp.concatenate(down_list, axis=0)))
    start_total = jnp.zeros((block_count, route_count, D), jnp.float32)
    stacked = (expert_ids, w_gate.reshape(EXPERTS, FF, D), w_up.reshape(EXPERTS, FF, D), w_down.reshape(EXPERTS, FF, D))
    route_total, (grad_gate, grad_up, grad_down) = lax.scan(one_expert, start_total, stacked)
    d_normed = lax.optimization_barrier(jnp.sum(route_total.reshape(SEQ, TOPK, D), axis=1))
    scaled_norm = norm_gain[None, :] * d_normed
    projection = lax.optimization_barrier(jnp.mean(state * scaled_norm, axis=1, keepdims=True))
    grad_state = (upstream_grad.astype(jnp.float32) + inv_rms * scaled_norm - state * inv_rms * inv_rms * inv_rms * projection).astype(jnp.bfloat16)
    dout = jnp.dot(grad_state, out_proj.T, preferred_element_type=jnp.float32).astype(jnp.bfloat16)

    def by_head(array):
        return array.reshape(SEQ, HEADS, HD).transpose(1, 0, 2)
    grad_query, grad_key, grad_value = lax.map(head_grads, (by_head(queries), by_head(key_rows), by_head(value_rows), by_head(dout)))

    def by_token(array):
        return array.transpose(1, 0, 2).reshape(SEQ, HEADS * HD)
    shape_out = (N_EP, N_CTX, HID_DEV, D)
    return (grad_state, by_token(grad_query), by_token(grad_key), by_token(grad_value), grad_gate.reshape(shape_out), grad_up.reshape(shape_out), grad_down.reshape(shape_out))
```

```python
import math

import jax
import jax.numpy as jnp
from jax import lax
from jax.sharding import PartitionSpec as P

HD = 128
EXP_DEV = 4


EPSILON = 1e-06
FLOOR_SCORE = -1e30
PRECISE = lax.Precision.HIGHEST


def shifted(block, axis, distance):
    devices = range(lax.axis_size(axis))
    route = [((i - distance) % len(devices), i) for i in devices]
    return lax.ppermute(block, axis, route)


def expert_pass(token_rows, grad_rows, gate_rows, up_rows, down_rows):
    contract = (((1,), (1,)), ((), ()))
    over_rows = (((0,), (0,)), ((), ()))
    pre_gate = lax.dot_general(token_rows, gate_rows, contract, preferred_element_type=jnp.float32)
    up_value = lax.dot_general(token_rows, up_rows, contract, preferred_element_type=jnp.float32)
    sigmoid = jax.nn.sigmoid(pre_gate)
    activation = (pre_gate * sigmoid * up_value).astype(jnp.bfloat16)
    act_grad = lax.dot_general(grad_rows, down_rows, contract, preferred_element_type=jnp.float32)
    up_grad = (act_grad * pre_gate * sigmoid).astype(jnp.bfloat16)
    gate_grad = (act_grad * up_value * sigmoid * (1.0 + pre_gate * (1.0 - sigmoid))).astype(
        jnp.bfloat16
    )
    partial_value = (
        jnp.dot(gate_grad, gate_rows, preferred_element_type=jnp.float32)
        + jnp.dot(up_grad, up_rows, preferred_element_type=jnp.float32)
    ).astype(jnp.bfloat16)
    gate_total = lax.dot_general(
        gate_grad, token_rows, over_rows, preferred_element_type=jnp.float32
    )
    up_total = lax.dot_general(up_grad, token_rows, over_rows, preferred_element_type=jnp.float32)
    down_total = lax.dot_general(
        activation, grad_rows, over_rows, preferred_element_type=jnp.float32
    )
    return (partial_value, gate_total, up_total, down_total)


def gather_rel(block, axis):
    count = lax.axis_size(axis)
    return [block] + [shifted(block, axis, d) for d in range(1, count)]


def local(
    hidden_state,
    upstream_grad,
    route_ids,
    route_gates,
    norm_gain,
    w_gate,
    w_up,
    w_down,
    out_proj,
    queries,
    key_rows,
    value_rows,
):
    ep_count = lax.axis_size("ep")
    ctx_count = lax.axis_size("ctx")
    tok_dev, model_width = hidden_state.shape
    topk_count = route_ids.shape[1]
    expert_count = EXP_DEV * ep_count
    copies = ctx_count // EXP_DEV
    capacity = max(2, 2 * tok_dev * topk_count // expert_count)
    route_count = tok_dev * topk_count
    tok_ctx = queries.shape[0]
    head_count = queries.shape[1] // HD
    ctx_index = lax.axis_index("ctx")
    ep_index = lax.axis_index("ep")
    scale = 1.0 / math.sqrt(HD)

    qkv_rel = gather_rel(jnp.stack([queries, key_rows, value_rows]), "ctx")
    block_pos = jnp.arange(tok_ctx, dtype=jnp.int32)
    rel_pos = jnp.concatenate(
        [((ctx_index - d) % ctx_count) * tok_ctx + block_pos for d in range(ctx_count)]
    )
    own_pos = ctx_index * tok_ctx + block_pos
    q_all = jnp.concatenate([b[0] for b in qkv_rel]).reshape(-1, head_count, HD)
    k_all = jnp.concatenate([b[1] for b in qkv_rel]).reshape(-1, head_count, HD)
    v_all = jnp.concatenate([b[2] for b in qkv_rel]).reshape(-1, head_count, HD)
    q_own = queries.reshape(tok_ctx, head_count, HD)
    k_own = key_rows.reshape(tok_ctx, head_count, HD)
    v_own = value_rows.reshape(tok_ctx, head_count, HD)

    raw_scores = jnp.einsum("qhd,khd->hqk", q_own, k_all, preferred_element_type=jnp.float32) * scale
    allowed = (own_pos[:, None] >= rel_pos[None, :])[None]
    row_top = jnp.max(jnp.where(allowed, raw_scores, FLOOR_SCORE), axis=2)
    row_total = jnp.sum(jnp.where(allowed, jnp.exp(raw_scores - row_top[:, :, None]), 0.0), axis=2)
    log_total = row_top + jnp.log(row_total)
    probs = jnp.where(allowed, jnp.exp(raw_scores - log_total[:, :, None]), 0.0)
    attn_out = jnp.einsum("hqk,khd->hqd", probs, v_all.astype(jnp.float32), precision=PRECISE)

    state = hidden_state.astype(jnp.float32)
    inv_rms = lax.rsqrt(jnp.mean(state * state, axis=1, keepdims=True) + EPSILON)
    normed = (state * inv_rms * norm_gain[None, :]).astype(jnp.bfloat16)
    flat_ids = route_ids.reshape(route_count)
    matches = (flat_ids[:, None] == jnp.arange(expert_count, dtype=jnp.int32)[None, :]).astype(
        jnp.int32
    )
    earlier = jnp.cumsum(matches, axis=0) - matches
    slot_index = jnp.sum(earlier * matches, axis=1)
    slot_ids = jnp.arange(capacity, dtype=jnp.int32)
    group_rel = (ep_index + jnp.arange(ep_count, dtype=jnp.int32)) % ep_count
    slot_rel = (ctx_index + jnp.arange(ctx_count, dtype=jnp.int32)) % ctx_count
    expert_of = group_rel[:, None] * EXP_DEV + (slot_rel // copies)[None, :]
    dispatch = (
        (flat_ids[None, None, None, :] == expert_of[:, :, None, None])
        & (slot_index[None, None, None, :] == slot_ids[None, None, :, None])
    ).astype(jnp.bfloat16)
    normed_rep = jnp.repeat(normed, topk_count, axis=0)
    upstream_rep = jnp.repeat(upstream_grad, topk_count, axis=0).astype(jnp.float32)
    scaled_grads = (route_gates.reshape(route_count, 1) * upstream_rep).astype(jnp.bfloat16)
    send_rows = jnp.einsum(
        "jpcr,rd->jpcd", dispatch, normed_rep, preferred_element_type=jnp.float32
    ).astype(jnp.bfloat16)
    send_grads = jnp.einsum(
        "jpcr,rd->jpcd", dispatch, scaled_grads, preferred_element_type=jnp.float32
    ).astype(jnp.bfloat16)
    send = jnp.stack([send_rows, send_grads], axis=2)
    recv_ep = jnp.stack(
        [send[0]] + [shifted(send[d], "ep", d) for d in range(1, ep_count)], axis=1
    )
    recv_ctx = jnp.stack(
        [recv_ep[0]] + [shifted(recv_ep[p], "ctx", p) for p in range(1, ctx_count)]
    )
    partial_value, gate_total, up_total, down_total = expert_pass(
        recv_ctx[:, :, 0].reshape(-1, model_width),
        recv_ctx[:, :, 1].reshape(-1, model_width),
        w_gate[0, 0],
        w_up[0, 0],
        w_down[0, 0],
    )
    partial_value = partial_value.reshape(ctx_count, ep_count, capacity, model_width)
    back_ctx = jnp.stack(
        [partial_value[0]]
        + [shifted(partial_value[p], "ctx", -p) for p in range(1, ctx_count)],
        axis=1,
    )
    back_ep = jnp.stack(
        [back_ctx[0]] + [shifted(back_ctx[d], "ep", -d) for d in range(1, ep_count)]
    )
    d_routes = jnp.einsum(
        "jpcd,jpcr->rd",
        back_ep.astype(jnp.float32),
        dispatch.astype(jnp.float32),
        precision=PRECISE,
    )
    d_normed = jnp.sum(d_routes.reshape(tok_dev, topk_count, model_width), axis=1)
    scaled_norm = norm_gain[None, :] * d_normed
    projection = jnp.mean(state * scaled_norm, axis=1, keepdims=True)
    grad_state = (
        upstream_grad.astype(jnp.float32)
        + inv_rms * scaled_norm
        - state * inv_rms * inv_rms * inv_rms * projection
    ).astype(jnp.bfloat16)
    state_rel = jnp.stack(gather_rel(grad_state, "ep"))
    state_block = jnp.take(
        state_rel, (ep_index - jnp.arange(ep_count, dtype=jnp.int32)) % ep_count, axis=0
    ).reshape(-1, model_width)
    dout = lax.dot_general(
        state_block, out_proj, (((1,), (1,)), ((), ())), preferred_element_type=jnp.float32
    ).astype(jnp.bfloat16)
    dout_own = dout.reshape(tok_ctx, head_count, HD)
    row_delta = jnp.einsum(
        "qhd,hqd->hq", dout_own.astype(jnp.float32), attn_out, precision=PRECISE
    )

    prob_grad = jnp.einsum("qhd,khd->hqk", dout_own, v_all, preferred_element_type=jnp.float32)
    score_grad = (probs * (prob_grad - row_delta[:, :, None])).astype(jnp.bfloat16)
    query_grad = (
        jnp.einsum("hqk,khd->qhd", score_grad, k_all, preferred_element_type=jnp.float32) * scale
    )

    dout_rel = gather_rel(dout, "ctx")
    stats_rel = gather_rel(jnp.stack([log_total, row_delta]), "ctx")
    dout_all = jnp.concatenate(dout_rel).reshape(-1, head_count, HD)
    log_all = jnp.concatenate([s[0] for s in stats_rel], axis=1)
    delta_all = jnp.concatenate([s[1] for s in stats_rel], axis=1)
    key_scores = jnp.einsum("qhd,khd->hqk", q_all, k_own, preferred_element_type=jnp.float32) * scale
    key_allowed = (rel_pos[:, None] >= own_pos[None, :])[None]
    key_probs = jnp.where(key_allowed, jnp.exp(key_scores - log_all[:, :, None]), 0.0)
    value_grad = jnp.einsum(
        "hqk,qhd->khd", key_probs.astype(jnp.bfloat16), dout_all, preferred_element_type=jnp.float32
    )
    key_prob_grad = jnp.einsum(
        "qhd,khd->hqk", dout_all, v_own, preferred_element_type=jnp.float32
    )
    key_score_grad = (key_probs * (key_prob_grad - delta_all[:, :, None])).astype(jnp.bfloat16)
    key_grad = (
        jnp.einsum("hqk,qhd->khd", key_score_grad, q_all, preferred_element_type=jnp.float32)
        * scale
    )
    flat_width = head_count * HD
    return (
        grad_state,
        query_grad.reshape(tok_ctx, flat_width).astype(jnp.bfloat16),
        key_grad.reshape(tok_ctx, flat_width).astype(jnp.bfloat16),
        value_grad.reshape(tok_ctx, flat_width).astype(jnp.bfloat16),
        gate_total.astype(jnp.bfloat16)[None, None],
        up_total.astype(jnp.bfloat16)[None, None],
        down_total.astype(jnp.bfloat16)[None, None],
    )


def solution(mesh):
    placed = (
        P(("ctx", "ep"), None),
        P(("ctx", "ep"), None),
        P(("ctx", "ep"), None),
        P(("ctx", "ep"), None),
        P(),
        P("ep", "ctx", None, None),
        P("ep", "ctx", None, None),
        P("ep", "ctx", None, None),
        P("ep", None),
        P("ctx", "ep"),
        P("ctx", "ep"),
        P("ctx", "ep"),
    )
    return jax.shard_map(
        local,
        mesh=mesh,
        in_specs=placed,
        out_specs=(
            P(("ctx", "ep"), None),
            P("ctx", "ep"),
            P("ctx", "ep"),
            P("ctx", "ep"),
            P("ep", "ctx", None, None),
            P("ep", "ctx", None, None),
            P("ep", "ctx", None, None),
        ),
        check_vma=False,
    )
```

```python
import math

import jax
import jax.numpy as jnp
from jax import lax
from jax.sharding import PartitionSpec as P

HD = 128
EXP_DEV = 4


EPSILON = 1e-06
FLOOR_SCORE = -1e30
PRECISE = lax.Precision.HIGHEST


def shifted(block, axis, distance):
    devices = range(lax.axis_size(axis))
    route = [((i - distance) % len(devices), i) for i in devices]
    return lax.ppermute(block, axis, route)


def expert_pass(token_rows, grad_rows, gate_rows, up_rows, down_rows):
    contract = (((1,), (1,)), ((), ()))
    over_rows = (((0,), (0,)), ((), ()))
    pre_gate = lax.dot_general(token_rows, gate_rows, contract, preferred_element_type=jnp.float32)
    up_value = lax.dot_general(token_rows, up_rows, contract, preferred_element_type=jnp.float32)
    sigmoid = jax.nn.sigmoid(pre_gate)
    activation = (pre_gate * sigmoid * up_value).astype(jnp.bfloat16)
    act_grad = lax.dot_general(grad_rows, down_rows, contract, preferred_element_type=jnp.float32)
    up_grad = (act_grad * pre_gate * sigmoid).astype(jnp.bfloat16)
    gate_grad = (act_grad * up_value * sigmoid * (1.0 + pre_gate * (1.0 - sigmoid))).astype(
        jnp.bfloat16
    )
    partial_value = (
        jnp.dot(gate_grad, gate_rows, preferred_element_type=jnp.float32)
        + jnp.dot(up_grad, up_rows, preferred_element_type=jnp.float32)
    ).astype(jnp.bfloat16)
    gate_total = lax.dot_general(
        gate_grad, token_rows, over_rows, preferred_element_type=jnp.float32
    )
    up_total = lax.dot_general(up_grad, token_rows, over_rows, preferred_element_type=jnp.float32)
    down_total = lax.dot_general(
        activation, grad_rows, over_rows, preferred_element_type=jnp.float32
    )
    return (partial_value, gate_total, up_total, down_total)


def gather_rel(block, axis):
    count = lax.axis_size(axis)
    return [block] + [shifted(block, axis, d) for d in range(1, count)]


def local(
    hidden_state,
    upstream_grad,
    route_ids,
    route_gates,
    norm_gain,
    w_gate,
    w_up,
    w_down,
    out_proj,
    queries,
    key_rows,
    value_rows,
):
    ep_count = lax.axis_size("ep")
    ctx_count = lax.axis_size("ctx")
    tok_dev, model_width = hidden_state.shape
    topk_count = route_ids.shape[1]
    expert_count = EXP_DEV * ep_count
    copies = ctx_count // EXP_DEV
    capacity = max(2, 2 * tok_dev * topk_count // expert_count)
    route_count = tok_dev * topk_count
    tok_ctx = queries.shape[0]
    head_count = queries.shape[1] // HD
    ctx_index = lax.axis_index("ctx")
    ep_index = lax.axis_index("ep")
    scale = 1.0 / math.sqrt(HD)

    qkv_rel = gather_rel(jnp.stack([queries, key_rows, value_rows]), "ctx")
    block_pos = jnp.arange(tok_ctx, dtype=jnp.int32)
    rel_pos = jnp.concatenate(
        [((ctx_index - d) % ctx_count) * tok_ctx + block_pos for d in range(ctx_count)]
    )
    own_pos = ctx_index * tok_ctx + block_pos
    q_all = jnp.concatenate([b[0] for b in qkv_rel]).reshape(-1, head_count, HD)
    k_all = jnp.concatenate([b[1] for b in qkv_rel]).reshape(-1, head_count, HD)
    v_all = jnp.concatenate([b[2] for b in qkv_rel]).reshape(-1, head_count, HD)
    q_own = queries.reshape(tok_ctx, head_count, HD)
    k_own = key_rows.reshape(tok_ctx, head_count, HD)
    v_own = value_rows.reshape(tok_ctx, head_count, HD)

    raw_scores = jnp.einsum("qhd,khd->hqk", q_own, k_all, preferred_element_type=jnp.float32) * scale
    allowed = (own_pos[:, None] >= rel_pos[None, :])[None]
    row_top = jnp.max(jnp.where(allowed, raw_scores, FLOOR_SCORE), axis=2)
    row_total = jnp.sum(jnp.where(allowed, jnp.exp(raw_scores - row_top[:, :, None]), 0.0), axis=2)
    log_total = row_top + jnp.log(row_total)
    probs = jnp.where(allowed, jnp.exp(raw_scores - log_total[:, :, None]), 0.0)
    attn_out = jnp.einsum("hqk,khd->hqd", probs, v_all.astype(jnp.float32), precision=PRECISE)

    state = hidden_state.astype(jnp.float32)
    inv_rms = lax.rsqrt(jnp.mean(state * state, axis=1, keepdims=True) + EPSILON)
    normed = (state * inv_rms * norm_gain[None, :]).astype(jnp.bfloat16)
    flat_ids = route_ids.reshape(route_count)
    matches = (flat_ids[:, None] == jnp.arange(expert_count, dtype=jnp.int32)[None, :]).astype(
        jnp.int32
    )
    earlier = jnp.cumsum(matches, axis=0) - matches
    slot_index = jnp.sum(earlier * matches, axis=1)
    slot_ids = jnp.arange(capacity, dtype=jnp.int32)
    group_rel = (ep_index + jnp.arange(ep_count, dtype=jnp.int32)) % ep_count
    slot_rel = (ctx_index + jnp.arange(ctx_count, dtype=jnp.int32)) % ctx_count
    expert_of = group_rel[:, None] * EXP_DEV + (slot_rel // copies)[None, :]
    dispatch = (
        (flat_ids[None, None, None, :] == expert_of[:, :, None, None])
        & (slot_index[None, None, None, :] == slot_ids[None, None, :, None])
    ).astype(jnp.bfloat16)
    normed_rep = jnp.repeat(normed, topk_count, axis=0)
    upstream_rep = jnp.repeat(upstream_grad, topk_count, axis=0).astype(jnp.float32)
    scaled_grads = (route_gates.reshape(route_count, 1) * upstream_rep).astype(jnp.bfloat16)
    send_rows = jnp.einsum(
        "jpcr,rd->jpcd", dispatch, normed_rep, preferred_element_type=jnp.float32
    ).astype(jnp.bfloat16)
    send_grads = jnp.einsum(
        "jpcr,rd->jpcd", dispatch, scaled_grads, preferred_element_type=jnp.float32
    ).astype(jnp.bfloat16)
    recv_ep = [
        jnp.concatenate(
            [send_rows[d].reshape(-1, model_width), send_grads[d].reshape(-1, model_width)]
        )
        for d in range(ep_count)
    ]
    recv_ep = [recv_ep[0]] + [shifted(recv_ep[d], "ep", d) for d in range(1, ep_count)]
    recv_ctx = [
        jnp.concatenate(
            [
                recv_ep[d].reshape(2, ctx_count, capacity, model_width)[pair, p]
                for pair in range(2)
                for d in range(ep_count)
            ]
        )
        for p in range(ctx_count)
    ]
    recv_ctx = [recv_ctx[0]] + [shifted(recv_ctx[p], "ctx", p) for p in range(1, ctx_count)]
    half = ep_count * capacity
    partial_value, gate_total, up_total, down_total = expert_pass(
        jnp.concatenate([blk[:half] for blk in recv_ctx]),
        jnp.concatenate([blk[half:] for blk in recv_ctx]),
        w_gate[0, 0],
        w_up[0, 0],
        w_down[0, 0],
    )
    back_ctx = [partial_value[p * half : (p + 1) * half] for p in range(ctx_count)]
    back_ctx = [back_ctx[0]] + [shifted(back_ctx[p], "ctx", -p) for p in range(1, ctx_count)]
    back_ep = [
        jnp.concatenate([blk[d * capacity : (d + 1) * capacity] for blk in back_ctx])
        for d in range(ep_count)
    ]
    back_ep = [back_ep[0]] + [shifted(back_ep[d], "ep", -d) for d in range(1, ep_count)]
    back_ep = jnp.stack(back_ep).reshape(ep_count, ctx_count, capacity, model_width)
    d_routes = jnp.einsum(
        "jpcd,jpcr->rd",
        back_ep.astype(jnp.float32),
        dispatch.astype(jnp.float32),
        precision=PRECISE,
    )
    d_normed = jnp.sum(d_routes.reshape(tok_dev, topk_count, model_width), axis=1)
    scaled_norm = norm_gain[None, :] * d_normed
    projection = jnp.mean(state * scaled_norm, axis=1, keepdims=True)
    grad_state = (
        upstream_grad.astype(jnp.float32)
        + inv_rms * scaled_norm
        - state * inv_rms * inv_rms * inv_rms * projection
    ).astype(jnp.bfloat16)
    state_rel = jnp.stack(gather_rel(grad_state, "ep"))
    state_block = jnp.take(
        state_rel, (ep_index - jnp.arange(ep_count, dtype=jnp.int32)) % ep_count, axis=0
    ).reshape(-1, model_width)
    dout = lax.dot_general(
        state_block, out_proj, (((1,), (1,)), ((), ())), preferred_element_type=jnp.float32
    ).astype(jnp.bfloat16)
    dout_own = dout.reshape(tok_ctx, head_count, HD)
    row_delta = jnp.einsum(
        "qhd,hqd->hq", dout_own.astype(jnp.float32), attn_out, precision=PRECISE
    )

    prob_grad = jnp.einsum("qhd,khd->hqk", dout_own, v_all, preferred_element_type=jnp.float32)
    score_grad = (probs * (prob_grad - row_delta[:, :, None])).astype(jnp.bfloat16)
    query_grad = (
        jnp.einsum("hqk,khd->qhd", score_grad, k_all, preferred_element_type=jnp.float32) * scale
    )

    dout_rel = gather_rel(dout, "ctx")
    stats_rel = gather_rel(jnp.stack([log_total, row_delta]), "ctx")
    dout_all = jnp.concatenate(dout_rel).reshape(-1, head_count, HD)
    log_all = jnp.concatenate([s[0] for s in stats_rel], axis=1)
    delta_all = jnp.concatenate([s[1] for s in stats_rel], axis=1)
    key_scores = jnp.einsum("qhd,khd->hqk", q_all, k_own, preferred_element_type=jnp.float32) * scale
    key_allowed = (rel_pos[:, None] >= own_pos[None, :])[None]
    key_probs = jnp.where(key_allowed, jnp.exp(key_scores - log_all[:, :, None]), 0.0)
    value_grad = jnp.einsum(
        "hqk,qhd->khd", key_probs.astype(jnp.bfloat16), dout_all, preferred_element_type=jnp.float32
    )
    key_prob_grad = jnp.einsum(
        "qhd,khd->hqk", dout_all, v_own, preferred_element_type=jnp.float32
    )
    key_score_grad = (key_probs * (key_prob_grad - delta_all[:, :, None])).astype(jnp.bfloat16)
    key_grad = (
        jnp.einsum("hqk,qhd->khd", key_score_grad, q_all, preferred_element_type=jnp.float32)
        * scale
    )
    flat_width = head_count * HD
    return (
        grad_state,
        query_grad.reshape(tok_ctx, flat_width).astype(jnp.bfloat16),
        key_grad.reshape(tok_ctx, flat_width).astype(jnp.bfloat16),
        value_grad.reshape(tok_ctx, flat_width).astype(jnp.bfloat16),
        gate_total.astype(jnp.bfloat16)[None, None],
        up_total.astype(jnp.bfloat16)[None, None],
        down_total.astype(jnp.bfloat16)[None, None],
    )


def solution(mesh):
    placed = (
        P(("ctx", "ep"), None),
        P(("ctx", "ep"), None),
        P(("ctx", "ep"), None),
        P(("ctx", "ep"), None),
        P(),
        P("ep", "ctx", None, None),
        P("ep", "ctx", None, None),
        P("ep", "ctx", None, None),
        P("ep", None),
        P("ctx", "ep"),
        P("ctx", "ep"),
        P("ctx", "ep"),
    )
    return jax.shard_map(
        local,
        mesh=mesh,
        in_specs=placed,
        out_specs=(
            P(("ctx", "ep"), None),
            P("ctx", "ep"),
            P("ctx", "ep"),
            P("ctx", "ep"),
            P("ep", "ctx", None, None),
            P("ep", "ctx", None, None),
            P("ep", "ctx", None, None),
        ),
        check_vma=False,
    )
```

```python
import math

import jax
import numpy as np
import jax.numpy as jnp
from jax import lax
from jax.sharding import PartitionSpec as P

HD = 128
EXP_DEV = 4


EPSILON = 1e-06
FLOOR_SCORE = -1e30
PRECISE = lax.Precision.HIGHEST


def shifted(block, axis, distance):
    devices = range(lax.axis_size(axis))
    route = [((i - distance) % len(devices), i) for i in devices]
    return lax.ppermute(block, axis, route)


def expert_pass(token_rows, grad_rows, gate_rows, up_rows, down_rows):
    contract = (((1,), (1,)), ((), ()))
    over_rows = (((0,), (0,)), ((), ()))
    pre_gate = lax.dot_general(token_rows, gate_rows, contract, preferred_element_type=jnp.float32)
    up_value = lax.dot_general(token_rows, up_rows, contract, preferred_element_type=jnp.float32)
    sigmoid = jax.nn.sigmoid(pre_gate)
    activation = (pre_gate * sigmoid * up_value).astype(jnp.bfloat16)
    act_grad = lax.dot_general(grad_rows, down_rows, contract, preferred_element_type=jnp.float32)
    up_grad = (act_grad * pre_gate * sigmoid).astype(jnp.bfloat16)
    gate_grad = (act_grad * up_value * sigmoid * (1.0 + pre_gate * (1.0 - sigmoid))).astype(
        jnp.bfloat16
    )
    partial_value = (
        jnp.dot(gate_grad, gate_rows, preferred_element_type=jnp.float32)
        + jnp.dot(up_grad, up_rows, preferred_element_type=jnp.float32)
    ).astype(jnp.bfloat16)
    gate_total = lax.dot_general(
        gate_grad, token_rows, over_rows, preferred_element_type=jnp.float32
    )
    up_total = lax.dot_general(up_grad, token_rows, over_rows, preferred_element_type=jnp.float32)
    down_total = lax.dot_general(
        activation, grad_rows, over_rows, preferred_element_type=jnp.float32
    )
    return (partial_value, gate_total, up_total, down_total)


def reorder_rows(rows, dims, order, chunks=1):
    count = int(np.prod(dims))
    source = np.transpose(np.arange(count).reshape(dims), order).reshape(-1)
    pick = (jnp.asarray(source, jnp.int32)[:, None] == jnp.arange(count, dtype=jnp.int32)[None, :])
    pick = pick.astype(rows.dtype)
    size = count // chunks
    out = [
        jnp.dot(pick[i * size : (i + 1) * size], rows, preferred_element_type=jnp.float32).astype(
            rows.dtype
        )
        for i in range(chunks)
    ]
    return out[0] if chunks == 1 else out


def gather_rel(block, axis):
    count = lax.axis_size(axis)
    return [block] + [shifted(block, axis, d) for d in range(1, count)]


def local(
    hidden_state,
    upstream_grad,
    route_ids,
    route_gates,
    norm_gain,
    w_gate,
    w_up,
    w_down,
    out_proj,
    queries,
    key_rows,
    value_rows,
):
    ep_count = lax.axis_size("ep")
    ctx_count = lax.axis_size("ctx")
    tok_dev, model_width = hidden_state.shape
    topk_count = route_ids.shape[1]
    expert_count = EXP_DEV * ep_count
    copies = ctx_count // EXP_DEV
    capacity = max(2, 2 * tok_dev * topk_count // expert_count)
    route_count = tok_dev * topk_count
    tok_ctx = queries.shape[0]
    head_count = queries.shape[1] // HD
    ctx_index = lax.axis_index("ctx")
    ep_index = lax.axis_index("ep")
    scale = 1.0 / math.sqrt(HD)

    qkv_rel = gather_rel(jnp.stack([queries, key_rows, value_rows]), "ctx")
    block_pos = jnp.arange(tok_ctx, dtype=jnp.int32)
    rel_pos = jnp.concatenate(
        [((ctx_index - d) % ctx_count) * tok_ctx + block_pos for d in range(ctx_count)]
    )
    own_pos = ctx_index * tok_ctx + block_pos
    q_all = jnp.concatenate([b[0] for b in qkv_rel]).reshape(-1, head_count, HD)
    k_all = jnp.concatenate([b[1] for b in qkv_rel]).reshape(-1, head_count, HD)
    v_all = jnp.concatenate([b[2] for b in qkv_rel]).reshape(-1, head_count, HD)
    q_own = queries.reshape(tok_ctx, head_count, HD)
    k_own = key_rows.reshape(tok_ctx, head_count, HD)
    v_own = value_rows.reshape(tok_ctx, head_count, HD)

    raw_scores = jnp.einsum("qhd,khd->hqk", q_own, k_all, preferred_element_type=jnp.float32) * scale
    allowed = (own_pos[:, None] >= rel_pos[None, :])[None]
    row_top = jnp.max(jnp.where(allowed, raw_scores, FLOOR_SCORE), axis=2)
    row_total = jnp.sum(jnp.where(allowed, jnp.exp(raw_scores - row_top[:, :, None]), 0.0), axis=2)
    log_total = row_top + jnp.log(row_total)
    probs = jnp.where(allowed, jnp.exp(raw_scores - log_total[:, :, None]), 0.0)
    attn_out = jnp.einsum("hqk,khd->hqd", probs, v_all.astype(jnp.float32), precision=PRECISE)

    state = hidden_state.astype(jnp.float32)
    inv_rms = lax.rsqrt(jnp.mean(state * state, axis=1, keepdims=True) + EPSILON)
    normed = (state * inv_rms * norm_gain[None, :]).astype(jnp.bfloat16)
    flat_ids = route_ids.reshape(route_count)
    matches = (flat_ids[:, None] == jnp.arange(expert_count, dtype=jnp.int32)[None, :]).astype(
        jnp.int32
    )
    earlier = jnp.cumsum(matches, axis=0) - matches
    slot_index = jnp.sum(earlier * matches, axis=1)
    slot_ids = jnp.arange(capacity, dtype=jnp.int32)
    group_rel = (ep_index + jnp.arange(ep_count, dtype=jnp.int32)) % ep_count
    slot_rel = (ctx_index + jnp.arange(ctx_count, dtype=jnp.int32)) % ctx_count
    expert_of = group_rel[:, None] * EXP_DEV + (slot_rel // copies)[None, :]
    routed = (flat_ids[None, None, None, :] == expert_of[:, :, None, None]) & (
        slot_index[None, None, None, :] == slot_ids[None, None, :, None]
    )
    pair_ids = jnp.arange(2, dtype=jnp.int32)
    choose = (pair_ids[None, :, None, None, None, None] == pair_ids[None, None, None, None, :, None]) & (
        routed[:, None, :, :, None, :]
    )
    choose = choose.reshape(ep_count * 2 * ctx_count * capacity, 2 * route_count)
    normed_rep = jnp.repeat(normed, topk_count, axis=0)
    upstream_rep = jnp.repeat(upstream_grad, topk_count, axis=0).astype(jnp.float32)
    scaled_grads = (route_gates.reshape(route_count, 1) * upstream_rep).astype(jnp.bfloat16)
    send_all = jnp.dot(
        choose.astype(jnp.bfloat16),
        jnp.concatenate([normed_rep, scaled_grads]),
        preferred_element_type=jnp.float32,
    ).astype(jnp.bfloat16)
    ep_rows = 2 * ctx_count * capacity
    recv_ep = [send_all[d * ep_rows : (d + 1) * ep_rows] for d in range(ep_count)]
    recv_ep = [recv_ep[0]] + [shifted(recv_ep[d], "ep", d) for d in range(1, ep_count)]
    regrouped = reorder_rows(
        jnp.concatenate(recv_ep), (ep_count, 2, ctx_count, capacity), (2, 1, 0, 3)
    )
    ctx_rows = 2 * ep_count * capacity
    recv_ctx = [regrouped[p * ctx_rows : (p + 1) * ctx_rows] for p in range(ctx_count)]
    recv_ctx = [recv_ctx[0]] + [shifted(recv_ctx[p], "ctx", p) for p in range(1, ctx_count)]
    half = ep_count * capacity
    partial_value, gate_total, up_total, down_total = expert_pass(
        jnp.concatenate([blk[:half] for blk in recv_ctx]),
        jnp.concatenate([blk[half:] for blk in recv_ctx]),
        w_gate[0, 0],
        w_up[0, 0],
        w_down[0, 0],
    )
    back_ctx = [partial_value[p * half : (p + 1) * half] for p in range(ctx_count)]
    back_ctx = [back_ctx[0]] + [shifted(back_ctx[p], "ctx", -p) for p in range(1, ctx_count)]
    back_ep = reorder_rows(
        jnp.concatenate(back_ctx), (ctx_count, ep_count, capacity), (1, 0, 2), ep_count
    )
    back_ep = [back_ep[0]] + [shifted(back_ep[d], "ep", -d) for d in range(1, ep_count)]
    to_token = jnp.sum(
        routed.reshape(ep_count, ctx_count * capacity, tok_dev, topk_count), axis=3
    ).astype(jnp.bfloat16)
    d_normed = sum(
        lax.dot_general(
            to_token[d], back_ep[d], (((0,), (0,)), ((), ())), preferred_element_type=jnp.float32
        )
        for d in range(ep_count)
    )
    scaled_norm = norm_gain[None, :] * d_normed
    projection = jnp.mean(state * scaled_norm, axis=1, keepdims=True)
    grad_state = (
        upstream_grad.astype(jnp.float32)
        + inv_rms * scaled_norm
        - state * inv_rms * inv_rms * inv_rms * projection
    ).astype(jnp.bfloat16)
    state_rel = jnp.stack(gather_rel(grad_state, "ep"))
    state_block = jnp.take(
        state_rel, (ep_index - jnp.arange(ep_count, dtype=jnp.int32)) % ep_count, axis=0
    ).reshape(-1, model_width)
    dout = lax.dot_general(
        state_block, out_proj, (((1,), (1,)), ((), ())), preferred_element_type=jnp.float32
    ).astype(jnp.bfloat16)
    dout_own = dout.reshape(tok_ctx, head_count, HD)
    row_delta = jnp.einsum(
        "qhd,hqd->hq", dout_own.astype(jnp.float32), attn_out, precision=PRECISE
    )

    prob_grad = jnp.einsum("qhd,khd->hqk", dout_own, v_all, preferred_element_type=jnp.float32)
    score_grad = (probs * (prob_grad - row_delta[:, :, None])).astype(jnp.bfloat16)
    query_grad = (
        jnp.einsum("hqk,khd->qhd", score_grad, k_all, preferred_element_type=jnp.float32) * scale
    )

    dout_rel = gather_rel(dout, "ctx")
    stats_rel = gather_rel(jnp.stack([log_total, row_delta]), "ctx")
    dout_all = jnp.concatenate(dout_rel).reshape(-1, head_count, HD)
    log_all = jnp.concatenate([s[0] for s in stats_rel], axis=1)
    delta_all = jnp.concatenate([s[1] for s in stats_rel], axis=1)
    key_scores = jnp.einsum("qhd,khd->hqk", q_all, k_own, preferred_element_type=jnp.float32) * scale
    key_allowed = (rel_pos[:, None] >= own_pos[None, :])[None]
    key_probs = jnp.where(key_allowed, jnp.exp(key_scores - log_all[:, :, None]), 0.0)
    value_grad = jnp.einsum(
        "hqk,qhd->khd", key_probs.astype(jnp.bfloat16), dout_all, preferred_element_type=jnp.float32
    )
    key_prob_grad = jnp.einsum(
        "qhd,khd->hqk", dout_all, v_own, preferred_element_type=jnp.float32
    )
    key_score_grad = (key_probs * (key_prob_grad - delta_all[:, :, None])).astype(jnp.bfloat16)
    key_grad = (
        jnp.einsum("hqk,qhd->khd", key_score_grad, q_all, preferred_element_type=jnp.float32)
        * scale
    )
    flat_width = head_count * HD
    return (
        grad_state,
        query_grad.reshape(tok_ctx, flat_width).astype(jnp.bfloat16),
        key_grad.reshape(tok_ctx, flat_width).astype(jnp.bfloat16),
        value_grad.reshape(tok_ctx, flat_width).astype(jnp.bfloat16),
        gate_total.astype(jnp.bfloat16)[None, None],
        up_total.astype(jnp.bfloat16)[None, None],
        down_total.astype(jnp.bfloat16)[None, None],
    )


def solution(mesh):
    placed = (
        P(("ctx", "ep"), None),
        P(("ctx", "ep"), None),
        P(("ctx", "ep"), None),
        P(("ctx", "ep"), None),
        P(),
        P("ep", "ctx", None, None),
        P("ep", "ctx", None, None),
        P("ep", "ctx", None, None),
        P("ep", None),
        P("ctx", "ep"),
        P("ctx", "ep"),
        P("ctx", "ep"),
    )
    return jax.shard_map(
        local,
        mesh=mesh,
        in_specs=placed,
        out_specs=(
            P(("ctx", "ep"), None),
            P("ctx", "ep"),
            P("ctx", "ep"),
            P("ctx", "ep"),
            P("ep", "ctx", None, None),
            P("ep", "ctx", None, None),
            P("ep", "ctx", None, None),
        ),
        check_vma=False,
    )
```

```python
import math

import jax
import numpy as np
import jax.numpy as jnp
from jax import lax
from jax.sharding import PartitionSpec as P

HD = 128
EXP_DEV = 4


EPSILON = 1e-06
FLOOR_SCORE = -1e30
PRECISE = lax.Precision.HIGHEST


def shifted(block, axis, distance):
    devices = range(lax.axis_size(axis))
    route = [((i - distance) % len(devices), i) for i in devices]
    return lax.ppermute(block, axis, route)


def expert_pass(token_rows, grad_rows, gate_rows, up_rows, down_rows):
    contract = (((1,), (1,)), ((), ()))
    over_rows = (((0,), (0,)), ((), ()))
    pre_gate = lax.dot_general(token_rows, gate_rows, contract, preferred_element_type=jnp.float32)
    up_value = lax.dot_general(token_rows, up_rows, contract, preferred_element_type=jnp.float32)
    sigmoid = jax.nn.sigmoid(pre_gate)
    activation = (pre_gate * sigmoid * up_value).astype(jnp.bfloat16)
    act_grad = lax.dot_general(grad_rows, down_rows, contract, preferred_element_type=jnp.float32)
    up_grad = (act_grad * pre_gate * sigmoid).astype(jnp.bfloat16)
    gate_grad = (act_grad * up_value * sigmoid * (1.0 + pre_gate * (1.0 - sigmoid))).astype(
        jnp.bfloat16
    )
    partial_value = (
        jnp.dot(gate_grad, gate_rows, preferred_element_type=jnp.float32)
        + jnp.dot(up_grad, up_rows, preferred_element_type=jnp.float32)
    ).astype(jnp.bfloat16)
    gate_total = lax.dot_general(
        gate_grad, token_rows, over_rows, preferred_element_type=jnp.float32
    )
    up_total = lax.dot_general(up_grad, token_rows, over_rows, preferred_element_type=jnp.float32)
    down_total = lax.dot_general(
        activation, grad_rows, over_rows, preferred_element_type=jnp.float32
    )
    return (partial_value, gate_total, up_total, down_total)


def reorder_rows(blocks, dims, order, chunks=1):
    count = int(np.prod(dims))
    source = np.transpose(np.arange(count).reshape(dims), order).reshape(-1)
    pick = (jnp.asarray(source, jnp.int32)[:, None] == jnp.arange(count, dtype=jnp.int32)[None, :])
    pick = pick.astype(blocks[0].dtype)
    size = count // chunks
    if count * blocks[0].shape[1] * 4 * len(blocks) > (32 << 20):
        blocks = [jnp.concatenate(blocks)]
    width = count // len(blocks)
    out = []
    for i in range(chunks):
        total = None
        for k, blk in enumerate(blocks):
            part = jnp.dot(
                pick[i * size : (i + 1) * size, k * width : (k + 1) * width],
                blk,
                preferred_element_type=jnp.float32,
            )
            total = part if total is None else total + part
        out.append(total.astype(blocks[0].dtype))
    return out[0] if chunks == 1 else out


def gather_rel(block, axis):
    count = lax.axis_size(axis)
    return [block] + [shifted(block, axis, d) for d in range(1, count)]


def local(
    hidden_state,
    upstream_grad,
    route_ids,
    route_gates,
    norm_gain,
    w_gate,
    w_up,
    w_down,
    out_proj,
    queries,
    key_rows,
    value_rows,
):
    ep_count = lax.axis_size("ep")
    ctx_count = lax.axis_size("ctx")
    tok_dev, model_width = hidden_state.shape
    topk_count = route_ids.shape[1]
    expert_count = EXP_DEV * ep_count
    copies = ctx_count // EXP_DEV
    capacity = max(2, 2 * tok_dev * topk_count // expert_count)
    route_count = tok_dev * topk_count
    tok_ctx = queries.shape[0]
    head_count = queries.shape[1] // HD
    ctx_index = lax.axis_index("ctx")
    ep_index = lax.axis_index("ep")
    scale = 1.0 / math.sqrt(HD)

    qkv_rel = gather_rel(jnp.stack([queries, key_rows, value_rows]), "ctx")
    block_pos = jnp.arange(tok_ctx, dtype=jnp.int32)
    rel_pos = jnp.concatenate(
        [((ctx_index - d) % ctx_count) * tok_ctx + block_pos for d in range(ctx_count)]
    )
    own_pos = ctx_index * tok_ctx + block_pos
    q_all = jnp.concatenate([b[0] for b in qkv_rel]).reshape(-1, head_count, HD)
    k_all = jnp.concatenate([b[1] for b in qkv_rel]).reshape(-1, head_count, HD)
    v_all = jnp.concatenate([b[2] for b in qkv_rel]).reshape(-1, head_count, HD)
    q_own = queries.reshape(tok_ctx, head_count, HD)
    k_own = key_rows.reshape(tok_ctx, head_count, HD)
    v_own = value_rows.reshape(tok_ctx, head_count, HD)

    raw_scores = jnp.einsum("qhd,khd->hqk", q_own, k_all, preferred_element_type=jnp.float32) * scale
    allowed = (own_pos[:, None] >= rel_pos[None, :])[None]
    row_top = jnp.max(jnp.where(allowed, raw_scores, FLOOR_SCORE), axis=2)
    row_total = jnp.sum(jnp.where(allowed, jnp.exp(raw_scores - row_top[:, :, None]), 0.0), axis=2)
    log_total = row_top + jnp.log(row_total)
    probs = jnp.where(allowed, jnp.exp(raw_scores - log_total[:, :, None]), 0.0)
    attn_out = jnp.einsum("hqk,khd->hqd", probs, v_all.astype(jnp.float32), precision=PRECISE)

    state = hidden_state.astype(jnp.float32)
    inv_rms = lax.rsqrt(jnp.mean(state * state, axis=1, keepdims=True) + EPSILON)
    normed = (state * inv_rms * norm_gain[None, :]).astype(jnp.bfloat16)
    flat_ids = route_ids.reshape(route_count)
    matches = (flat_ids[:, None] == jnp.arange(expert_count, dtype=jnp.int32)[None, :]).astype(
        jnp.int32
    )
    earlier = jnp.cumsum(matches, axis=0) - matches
    slot_index = jnp.sum(earlier * matches, axis=1)
    slot_ids = jnp.arange(capacity, dtype=jnp.int32)
    group_rel = (ep_index + jnp.arange(ep_count, dtype=jnp.int32)) % ep_count
    slot_rel = (ctx_index + jnp.arange(ctx_count, dtype=jnp.int32)) % ctx_count
    expert_of = group_rel[:, None] * EXP_DEV + (slot_rel // copies)[None, :]
    routed = (flat_ids[None, None, None, :] == expert_of[:, :, None, None]) & (
        slot_index[None, None, None, :] == slot_ids[None, None, :, None]
    )
    pair_ids = jnp.arange(2, dtype=jnp.int32)
    choose = (pair_ids[None, :, None, None, None, None] == pair_ids[None, None, None, None, :, None]) & (
        routed[:, None, :, :, None, :]
    )
    choose = choose.reshape(ep_count * 2 * ctx_count * capacity, 2 * route_count)
    normed_rep = jnp.repeat(normed, topk_count, axis=0)
    upstream_rep = jnp.repeat(upstream_grad, topk_count, axis=0).astype(jnp.float32)
    scaled_grads = (route_gates.reshape(route_count, 1) * upstream_rep).astype(jnp.bfloat16)
    send_all = jnp.dot(
        choose.astype(jnp.bfloat16),
        jnp.concatenate([normed_rep, scaled_grads]),
        preferred_element_type=jnp.float32,
    ).astype(jnp.bfloat16)
    ep_rows = 2 * ctx_count * capacity
    recv_ep = [send_all[d * ep_rows : (d + 1) * ep_rows] for d in range(ep_count)]
    recv_ep = [recv_ep[0]] + [shifted(recv_ep[d], "ep", d) for d in range(1, ep_count)]
    regrouped = reorder_rows(
        recv_ep, (ep_count, 2, ctx_count, capacity), (2, 1, 0, 3)
    )
    ctx_rows = 2 * ep_count * capacity
    recv_ctx = [regrouped[p * ctx_rows : (p + 1) * ctx_rows] for p in range(ctx_count)]
    recv_ctx = [recv_ctx[0]] + [shifted(recv_ctx[p], "ctx", p) for p in range(1, ctx_count)]
    half = ep_count * capacity
    partial_value, gate_total, up_total, down_total = expert_pass(
        jnp.concatenate([blk[:half] for blk in recv_ctx]),
        jnp.concatenate([blk[half:] for blk in recv_ctx]),
        w_gate[0, 0],
        w_up[0, 0],
        w_down[0, 0],
    )
    back_ctx = [partial_value[p * half : (p + 1) * half] for p in range(ctx_count)]
    back_ctx = [back_ctx[0]] + [shifted(back_ctx[p], "ctx", -p) for p in range(1, ctx_count)]
    back_ep = reorder_rows(
        back_ctx, (ctx_count, ep_count, capacity), (1, 0, 2), ep_count
    )
    back_ep = [back_ep[0]] + [shifted(back_ep[d], "ep", -d) for d in range(1, ep_count)]
    to_token = jnp.sum(
        routed.reshape(ep_count, ctx_count * capacity, tok_dev, topk_count), axis=3
    ).astype(jnp.bfloat16)
    d_normed = sum(
        lax.dot_general(
            to_token[d], back_ep[d], (((0,), (0,)), ((), ())), preferred_element_type=jnp.float32
        )
        for d in range(ep_count)
    )
    scaled_norm = norm_gain[None, :] * d_normed
    projection = jnp.mean(state * scaled_norm, axis=1, keepdims=True)
    grad_state = (
        upstream_grad.astype(jnp.float32)
        + inv_rms * scaled_norm
        - state * inv_rms * inv_rms * inv_rms * projection
    ).astype(jnp.bfloat16)
    state_rel = jnp.stack(gather_rel(grad_state, "ep"))
    state_block = jnp.take(
        state_rel, (ep_index - jnp.arange(ep_count, dtype=jnp.int32)) % ep_count, axis=0
    ).reshape(-1, model_width)
    dout = lax.dot_general(
        state_block, out_proj, (((1,), (1,)), ((), ())), preferred_element_type=jnp.float32
    ).astype(jnp.bfloat16)
    dout_own = dout.reshape(tok_ctx, head_count, HD)
    row_delta = jnp.einsum(
        "qhd,hqd->hq", dout_own.astype(jnp.float32), attn_out, precision=PRECISE
    )

    prob_grad = jnp.einsum("qhd,khd->hqk", dout_own, v_all, preferred_element_type=jnp.float32)
    score_grad = (probs * (prob_grad - row_delta[:, :, None])).astype(jnp.bfloat16)
    query_grad = (
        jnp.einsum("hqk,khd->qhd", score_grad, k_all, preferred_element_type=jnp.float32) * scale
    )

    dout_rel = gather_rel(dout, "ctx")
    stats_rel = gather_rel(jnp.stack([log_total, row_delta]), "ctx")
    dout_all = jnp.concatenate(dout_rel).reshape(-1, head_count, HD)
    log_all = jnp.concatenate([s[0] for s in stats_rel], axis=1)
    delta_all = jnp.concatenate([s[1] for s in stats_rel], axis=1)
    key_scores = jnp.einsum("qhd,khd->hqk", q_all, k_own, preferred_element_type=jnp.float32) * scale
    key_allowed = (rel_pos[:, None] >= own_pos[None, :])[None]
    key_probs = jnp.where(key_allowed, jnp.exp(key_scores - log_all[:, :, None]), 0.0)
    value_grad = jnp.einsum(
        "hqk,qhd->khd", key_probs.astype(jnp.bfloat16), dout_all, preferred_element_type=jnp.float32
    )
    key_prob_grad = jnp.einsum(
        "qhd,khd->hqk", dout_all, v_own, preferred_element_type=jnp.float32
    )
    key_score_grad = (key_probs * (key_prob_grad - delta_all[:, :, None])).astype(jnp.bfloat16)
    key_grad = (
        jnp.einsum("hqk,qhd->khd", key_score_grad, q_all, preferred_element_type=jnp.float32)
        * scale
    )
    flat_width = head_count * HD
    return (
        grad_state,
        query_grad.reshape(tok_ctx, flat_width).astype(jnp.bfloat16),
        key_grad.reshape(tok_ctx, flat_width).astype(jnp.bfloat16),
        value_grad.reshape(tok_ctx, flat_width).astype(jnp.bfloat16),
        gate_total.astype(jnp.bfloat16)[None, None],
        up_total.astype(jnp.bfloat16)[None, None],
        down_total.astype(jnp.bfloat16)[None, None],
    )


def solution(mesh):
    placed = (
        P(("ctx", "ep"), None),
        P(("ctx", "ep"), None),
        P(("ctx", "ep"), None),
        P(("ctx", "ep"), None),
        P(),
        P("ep", "ctx", None, None),
        P("ep", "ctx", None, None),
        P("ep", "ctx", None, None),
        P("ep", None),
        P("ctx", "ep"),
        P("ctx", "ep"),
        P("ctx", "ep"),
    )
    return jax.shard_map(
        local,
        mesh=mesh,
        in_specs=placed,
        out_specs=(
            P(("ctx", "ep"), None),
            P("ctx", "ep"),
            P("ctx", "ep"),
            P("ctx", "ep"),
            P("ep", "ctx", None, None),
            P("ep", "ctx", None, None),
            P("ep", "ctx", None, None),
        ),
        check_vma=False,
    )
```

```python
import math

import jax
import numpy as np
import jax.numpy as jnp
from jax import lax
from jax.sharding import PartitionSpec as P

HD = 128
EXP_DEV = 4


EPSILON = 1e-06
FLOOR_SCORE = -1e30
PRECISE = lax.Precision.HIGHEST


def shifted(block, axis, distance):
    devices = range(lax.axis_size(axis))
    route = [((i - distance) % len(devices), i) for i in devices]
    return lax.ppermute(block, axis, route)


def expert_pass(token_rows, grad_rows, gate_rows, up_rows, down_rows):
    contract = (((1,), (1,)), ((), ()))
    over_rows = (((0,), (0,)), ((), ()))
    pre_gate = lax.dot_general(token_rows, gate_rows, contract, preferred_element_type=jnp.float32)
    up_value = lax.dot_general(token_rows, up_rows, contract, preferred_element_type=jnp.float32)
    sigmoid = jax.nn.sigmoid(pre_gate)
    activation = (pre_gate * sigmoid * up_value).astype(jnp.bfloat16)
    act_grad = lax.dot_general(grad_rows, down_rows, contract, preferred_element_type=jnp.float32)
    up_grad = (act_grad * pre_gate * sigmoid).astype(jnp.bfloat16)
    gate_grad = (act_grad * up_value * sigmoid * (1.0 + pre_gate * (1.0 - sigmoid))).astype(
        jnp.bfloat16
    )
    partial_value = (
        jnp.dot(gate_grad, gate_rows, preferred_element_type=jnp.float32)
        + jnp.dot(up_grad, up_rows, preferred_element_type=jnp.float32)
    ).astype(jnp.bfloat16)
    gate_total = lax.dot_general(
        gate_grad, token_rows, over_rows, preferred_element_type=jnp.float32
    )
    up_total = lax.dot_general(up_grad, token_rows, over_rows, preferred_element_type=jnp.float32)
    down_total = lax.dot_general(
        activation, grad_rows, over_rows, preferred_element_type=jnp.float32
    )
    return (partial_value, gate_total, up_total, down_total)


def reorder_rows(blocks, dims, order, chunks=1):
    count = int(np.prod(dims))
    source = np.transpose(np.arange(count).reshape(dims), order).reshape(-1)
    pick = (jnp.asarray(source, jnp.int32)[:, None] == jnp.arange(count, dtype=jnp.int32)[None, :])
    pick = pick.astype(blocks[0].dtype)
    size = count // chunks
    if count * blocks[0].shape[1] * 4 * len(blocks) > (32 << 20):
        blocks = [jnp.concatenate(blocks)]
    width = count // len(blocks)
    out = []
    for i in range(chunks):
        total = None
        for k, blk in enumerate(blocks):
            part = jnp.dot(
                pick[i * size : (i + 1) * size, k * width : (k + 1) * width],
                blk,
                preferred_element_type=jnp.float32,
            )
            total = part if total is None else total + part
        out.append(total.astype(blocks[0].dtype))
    return out[0] if chunks == 1 else out


def gather_rel(block, axis):
    count = lax.axis_size(axis)
    return [block] + [shifted(block, axis, d) for d in range(1, count)]


def local(
    hidden_state,
    upstream_grad,
    route_ids,
    route_gates,
    norm_gain,
    w_gate,
    w_up,
    w_down,
    out_proj,
    queries,
    key_rows,
    value_rows,
):
    ep_count = lax.axis_size("ep")
    ctx_count = lax.axis_size("ctx")
    tok_dev, model_width = hidden_state.shape
    topk_count = route_ids.shape[1]
    expert_count = EXP_DEV * ep_count
    copies = ctx_count // EXP_DEV
    capacity = max(2, 2 * tok_dev * topk_count // expert_count)
    route_count = tok_dev * topk_count
    tok_ctx = queries.shape[0]
    head_count = queries.shape[1] // HD
    ctx_index = lax.axis_index("ctx")
    ep_index = lax.axis_index("ep")
    scale = 1.0 / math.sqrt(HD)

    qkv_rel = gather_rel(jnp.stack([queries, key_rows, value_rows]), "ctx")
    block_pos = jnp.arange(tok_ctx, dtype=jnp.int32)
    rel_pos = jnp.concatenate(
        [((ctx_index - d) % ctx_count) * tok_ctx + block_pos for d in range(ctx_count)]
    )
    own_pos = ctx_index * tok_ctx + block_pos
    q_all = jnp.concatenate([b[0] for b in qkv_rel]).reshape(-1, head_count, HD)
    k_all = jnp.concatenate([b[1] for b in qkv_rel]).reshape(-1, head_count, HD)
    v_all = jnp.concatenate([b[2] for b in qkv_rel]).reshape(-1, head_count, HD)
    q_own = queries.reshape(tok_ctx, head_count, HD)
    k_own = key_rows.reshape(tok_ctx, head_count, HD)
    v_own = value_rows.reshape(tok_ctx, head_count, HD)

    raw_scores = jnp.einsum("qhd,khd->hqk", q_own, k_all, preferred_element_type=jnp.float32) * scale
    allowed = (own_pos[:, None] >= rel_pos[None, :])[None]
    row_top = jnp.max(jnp.where(allowed, raw_scores, FLOOR_SCORE), axis=2)
    row_total = jnp.sum(jnp.where(allowed, jnp.exp(raw_scores - row_top[:, :, None]), 0.0), axis=2)
    log_total = row_top + jnp.log(row_total)
    probs = jnp.where(allowed, jnp.exp(raw_scores - log_total[:, :, None]), 0.0)
    attn_out = jnp.einsum("hqk,khd->hqd", probs, v_all.astype(jnp.float32), precision=PRECISE)

    state = hidden_state.astype(jnp.float32)
    inv_rms = lax.rsqrt(jnp.mean(state * state, axis=1, keepdims=True) + EPSILON)
    normed = (state * inv_rms * norm_gain[None, :]).astype(jnp.bfloat16)
    flat_ids = route_ids.reshape(route_count)
    matches = (flat_ids[:, None] == jnp.arange(expert_count, dtype=jnp.int32)[None, :]).astype(
        jnp.int32
    )
    earlier = jnp.cumsum(matches, axis=0) - matches
    slot_index = jnp.sum(earlier * matches, axis=1)
    slot_ids = jnp.arange(capacity, dtype=jnp.int32)
    group_rel = (ep_index + jnp.arange(ep_count, dtype=jnp.int32)) % ep_count
    slot_rel = (ctx_index + jnp.arange(ctx_count, dtype=jnp.int32)) % ctx_count
    expert_of = group_rel[:, None] * EXP_DEV + (slot_rel // copies)[None, :]
    routed = (flat_ids[None, None, None, :] == expert_of[:, :, None, None]) & (
        slot_index[None, None, None, :] == slot_ids[None, None, :, None]
    )
    gate_hi = lax.reduce_precision(route_gates, exponent_bits=8, mantissa_bits=7)
    gate_rest = route_gates - gate_hi
    gate_mid = lax.reduce_precision(gate_rest, exponent_bits=8, mantissa_bits=7)
    gate_lo = (gate_rest - gate_mid).astype(jnp.bfloat16)
    gate_hi = gate_hi.astype(jnp.bfloat16)
    gate_mid = gate_mid.astype(jnp.bfloat16)
    meta = jnp.concatenate(
        [
            route_ids.astype(jnp.bfloat16).reshape(-1),
            gate_hi.reshape(-1),
            gate_mid.reshape(-1),
            gate_lo.reshape(-1),
        ]
    )
    meta = jnp.pad(meta, (0, model_width - meta.shape[0]))[None]
    payload = jnp.concatenate([normed, upstream_grad, meta])
    recv_ep = [payload] + [shifted(payload, "ep", d) for d in range(1, ep_count)]
    metas = jnp.stack([blk[2 * tok_dev] for blk in recv_ep]).astype(jnp.float32)
    in_ids = metas[:, :route_count].astype(jnp.int32)
    in_gates = (
        metas[:, route_count : 2 * route_count]
        + metas[:, 2 * route_count : 3 * route_count]
        + metas[:, 3 * route_count : 4 * route_count]
    )
    in_matches = (in_ids[:, :, None] == jnp.arange(expert_count, dtype=jnp.int32)[None, None, :]).astype(
        jnp.int32
    )
    in_slots = jnp.sum((jnp.cumsum(in_matches, axis=1) - in_matches) * in_matches, axis=2)
    own_experts = ep_index * EXP_DEV + slot_rel // copies
    in_routed = (in_ids[None, :, None, :] == own_experts[:, None, None, None]) & (
        in_slots[None, :, None, :] == slot_ids[None, None, :, None]
    )
    gate_row = jnp.sum(jnp.where(in_routed, in_gates[None, :, None, :], 0.0), axis=3)
    pick_token = jnp.sum(
        in_routed.reshape(ctx_count, ep_count, capacity, tok_dev, topk_count), axis=4
    )
    same_source = jnp.arange(ep_count)[:, None] == jnp.arange(ep_count)[None, :]
    pick_token = jnp.where(
        same_source[None, :, None, :, None], pick_token[:, :, :, None, :], 0
    ).reshape(ctx_count, ep_count * capacity, ep_count * tok_dev).astype(jnp.bfloat16)
    tokens_normed = jnp.concatenate([blk[:tok_dev] for blk in recv_ep])
    tokens_up = jnp.concatenate([blk[tok_dev : 2 * tok_dev] for blk in recv_ep])
    regrouped = []
    for p in range(ctx_count):
        rows_x = jnp.dot(pick_token[p], tokens_normed, preferred_element_type=jnp.float32)
        rows_up = jnp.dot(pick_token[p], tokens_up, preferred_element_type=jnp.float32)
        rows_g = gate_row[p].reshape(-1, 1) * rows_up
        regrouped.append(
            jnp.concatenate([rows_x.astype(jnp.bfloat16), rows_g.astype(jnp.bfloat16)])
        )
    recv_ctx = regrouped
    recv_ctx = [recv_ctx[0]] + [shifted(recv_ctx[p], "ctx", p) for p in range(1, ctx_count)]
    half = ep_count * capacity
    partial_value, gate_total, up_total, down_total = expert_pass(
        jnp.concatenate([blk[:half] for blk in recv_ctx]),
        jnp.concatenate([blk[half:] for blk in recv_ctx]),
        w_gate[0, 0],
        w_up[0, 0],
        w_down[0, 0],
    )
    back_ctx = [partial_value[p * half : (p + 1) * half] for p in range(ctx_count)]
    back_ctx = [back_ctx[0]] + [shifted(back_ctx[p], "ctx", -p) for p in range(1, ctx_count)]
    back_ep = reorder_rows(
        back_ctx, (ctx_count, ep_count, capacity), (1, 0, 2), ep_count
    )
    back_ep = [back_ep[0]] + [shifted(back_ep[d], "ep", -d) for d in range(1, ep_count)]
    to_token = jnp.sum(
        routed.reshape(ep_count, ctx_count * capacity, tok_dev, topk_count), axis=3
    ).astype(jnp.bfloat16)
    d_normed = sum(
        lax.dot_general(
            to_token[d], back_ep[d], (((0,), (0,)), ((), ())), preferred_element_type=jnp.float32
        )
        for d in range(ep_count)
    )
    scaled_norm = norm_gain[None, :] * d_normed
    projection = jnp.mean(state * scaled_norm, axis=1, keepdims=True)
    grad_state = (
        upstream_grad.astype(jnp.float32)
        + inv_rms * scaled_norm
        - state * inv_rms * inv_rms * inv_rms * projection
    ).astype(jnp.bfloat16)
    state_rel = jnp.stack(gather_rel(grad_state, "ep"))
    state_block = jnp.take(
        state_rel, (ep_index - jnp.arange(ep_count, dtype=jnp.int32)) % ep_count, axis=0
    ).reshape(-1, model_width)
    dout = lax.dot_general(
        state_block, out_proj, (((1,), (1,)), ((), ())), preferred_element_type=jnp.float32
    ).astype(jnp.bfloat16)
    dout_own = dout.reshape(tok_ctx, head_count, HD)
    row_delta = jnp.einsum(
        "qhd,hqd->hq", dout_own.astype(jnp.float32), attn_out, precision=PRECISE
    )

    prob_grad = jnp.einsum("qhd,khd->hqk", dout_own, v_all, preferred_element_type=jnp.float32)
    score_grad = (probs * (prob_grad - row_delta[:, :, None])).astype(jnp.bfloat16)
    query_grad = (
        jnp.einsum("hqk,khd->qhd", score_grad, k_all, preferred_element_type=jnp.float32) * scale
    )

    dout_rel = gather_rel(dout, "ctx")
    stats_rel = gather_rel(jnp.stack([log_total, row_delta]), "ctx")
    dout_all = jnp.concatenate(dout_rel).reshape(-1, head_count, HD)
    log_all = jnp.concatenate([s[0] for s in stats_rel], axis=1)
    delta_all = jnp.concatenate([s[1] for s in stats_rel], axis=1)
    key_scores = jnp.einsum("qhd,khd->hqk", q_all, k_own, preferred_element_type=jnp.float32) * scale
    key_allowed = (rel_pos[:, None] >= own_pos[None, :])[None]
    key_probs = jnp.where(key_allowed, jnp.exp(key_scores - log_all[:, :, None]), 0.0)
    value_grad = jnp.einsum(
        "hqk,qhd->khd", key_probs.astype(jnp.bfloat16), dout_all, preferred_element_type=jnp.float32
    )
    key_prob_grad = jnp.einsum(
        "qhd,khd->hqk", dout_all, v_own, preferred_element_type=jnp.float32
    )
    key_score_grad = (key_probs * (key_prob_grad - delta_all[:, :, None])).astype(jnp.bfloat16)
    key_grad = (
        jnp.einsum("hqk,qhd->khd", key_score_grad, q_all, preferred_element_type=jnp.float32)
        * scale
    )
    flat_width = head_count * HD
    return (
        grad_state,
        query_grad.reshape(tok_ctx, flat_width).astype(jnp.bfloat16),
        key_grad.reshape(tok_ctx, flat_width).astype(jnp.bfloat16),
        value_grad.reshape(tok_ctx, flat_width).astype(jnp.bfloat16),
        gate_total.astype(jnp.bfloat16)[None, None],
        up_total.astype(jnp.bfloat16)[None, None],
        down_total.astype(jnp.bfloat16)[None, None],
    )


def solution(mesh):
    placed = (
        P(("ctx", "ep"), None),
        P(("ctx", "ep"), None),
        P(("ctx", "ep"), None),
        P(("ctx", "ep"), None),
        P(),
        P("ep", "ctx", None, None),
        P("ep", "ctx", None, None),
        P("ep", "ctx", None, None),
        P("ep", None),
        P("ctx", "ep"),
        P("ctx", "ep"),
        P("ctx", "ep"),
    )
    return jax.shard_map(
        local,
        mesh=mesh,
        in_specs=placed,
        out_specs=(
            P(("ctx", "ep"), None),
            P("ctx", "ep"),
            P("ctx", "ep"),
            P("ctx", "ep"),
            P("ep", "ctx", None, None),
            P("ep", "ctx", None, None),
            P("ep", "ctx", None, None),
        ),
        check_vma=False,
    )
```

```python
import math

import jax
import numpy as np
import jax.numpy as jnp
from jax import lax
from jax.sharding import PartitionSpec as P

HD = 128
EXP_DEV = 4


EPSILON = 1e-06
FLOOR_SCORE = -1e30
PRECISE = lax.Precision.HIGHEST


def shifted(block, axis, distance):
    devices = range(lax.axis_size(axis))
    route = [((i - distance) % len(devices), i) for i in devices]
    return lax.ppermute(block, axis, route)


def expert_pass(token_rows, grad_rows, gate_rows, up_rows, down_rows):
    contract = (((1,), (1,)), ((), ()))
    pre_gate = lax.dot_general(token_rows, gate_rows, contract, preferred_element_type=jnp.float32)
    up_value = lax.dot_general(token_rows, up_rows, contract, preferred_element_type=jnp.float32)
    sigmoid = jax.nn.sigmoid(pre_gate)
    activation = (pre_gate * sigmoid * up_value).astype(jnp.bfloat16)
    act_grad = lax.dot_general(grad_rows, down_rows, contract, preferred_element_type=jnp.float32)
    up_grad = (act_grad * pre_gate * sigmoid).astype(jnp.bfloat16)
    gate_grad = (act_grad * up_value * sigmoid * (1.0 + pre_gate * (1.0 - sigmoid))).astype(
        jnp.bfloat16
    )
    partial_value = (
        jnp.dot(gate_grad, gate_rows, preferred_element_type=jnp.float32)
        + jnp.dot(up_grad, up_rows, preferred_element_type=jnp.float32)
    ).astype(jnp.bfloat16)
    return (partial_value, (gate_grad, up_grad, activation))


def weight_grads(token_rows, grad_rows, gate_grad, up_grad, activation):
    over_rows = (((0,), (0,)), ((), ()))
    gate_total = lax.dot_general(
        gate_grad, token_rows, over_rows, preferred_element_type=jnp.float32
    )
    up_total = lax.dot_general(up_grad, token_rows, over_rows, preferred_element_type=jnp.float32)
    down_total = lax.dot_general(
        activation, grad_rows, over_rows, preferred_element_type=jnp.float32
    )
    return (gate_total, up_total, down_total)


def reorder_rows(blocks, dims, order, chunks=1):
    count = int(np.prod(dims))
    source = np.transpose(np.arange(count).reshape(dims), order).reshape(-1)
    pick = (jnp.asarray(source, jnp.int32)[:, None] == jnp.arange(count, dtype=jnp.int32)[None, :])
    pick = pick.astype(blocks[0].dtype)
    size = count // chunks
    if count * blocks[0].shape[1] * 4 * len(blocks) > (32 << 20):
        blocks = [jnp.concatenate(blocks)]
    width = count // len(blocks)
    out = []
    for i in range(chunks):
        total = None
        for k, blk in enumerate(blocks):
            part = jnp.dot(
                pick[i * size : (i + 1) * size, k * width : (k + 1) * width],
                blk,
                preferred_element_type=jnp.float32,
            )
            total = part if total is None else total + part
        out.append(total.astype(blocks[0].dtype))
    return out[0] if chunks == 1 else out


def gather_rel(block, axis):
    count = lax.axis_size(axis)
    return [block] + [shifted(block, axis, d) for d in range(1, count)]


def local(
    hidden_state,
    upstream_grad,
    route_ids,
    route_gates,
    norm_gain,
    w_gate,
    w_up,
    w_down,
    out_proj,
    queries,
    key_rows,
    value_rows,
):
    ep_count = lax.axis_size("ep")
    ctx_count = lax.axis_size("ctx")
    tok_dev, model_width = hidden_state.shape
    topk_count = route_ids.shape[1]
    expert_count = EXP_DEV * ep_count
    copies = ctx_count // EXP_DEV
    capacity = max(2, 2 * tok_dev * topk_count // expert_count)
    route_count = tok_dev * topk_count
    tok_ctx = queries.shape[0]
    head_count = queries.shape[1] // HD
    ctx_index = lax.axis_index("ctx")
    ep_index = lax.axis_index("ep")
    scale = 1.0 / math.sqrt(HD)

    qkv_rel = gather_rel(jnp.stack([queries, key_rows, value_rows]), "ctx")
    block_pos = jnp.arange(tok_ctx, dtype=jnp.int32)
    rel_pos = jnp.concatenate(
        [((ctx_index - d) % ctx_count) * tok_ctx + block_pos for d in range(ctx_count)]
    )
    own_pos = ctx_index * tok_ctx + block_pos
    q_all = jnp.concatenate([b[0] for b in qkv_rel]).reshape(-1, head_count, HD)
    k_all = jnp.concatenate([b[1] for b in qkv_rel]).reshape(-1, head_count, HD)
    v_all = jnp.concatenate([b[2] for b in qkv_rel]).reshape(-1, head_count, HD)
    q_own = queries.reshape(tok_ctx, head_count, HD)
    k_own = key_rows.reshape(tok_ctx, head_count, HD)
    v_own = value_rows.reshape(tok_ctx, head_count, HD)

    raw_scores = jnp.einsum("qhd,khd->hqk", q_own, k_all, preferred_element_type=jnp.float32) * scale
    allowed = (own_pos[:, None] >= rel_pos[None, :])[None]
    row_top = jnp.max(jnp.where(allowed, raw_scores, FLOOR_SCORE), axis=2)
    row_total = jnp.sum(jnp.where(allowed, jnp.exp(raw_scores - row_top[:, :, None]), 0.0), axis=2)
    log_total = row_top + jnp.log(row_total)
    probs = jnp.where(allowed, jnp.exp(raw_scores - log_total[:, :, None]), 0.0)
    attn_out = jnp.einsum("hqk,khd->hqd", probs, v_all.astype(jnp.float32), precision=PRECISE)

    state = hidden_state.astype(jnp.float32)
    inv_rms = lax.rsqrt(jnp.mean(state * state, axis=1, keepdims=True) + EPSILON)
    normed = (state * inv_rms * norm_gain[None, :]).astype(jnp.bfloat16)
    flat_ids = route_ids.reshape(route_count)
    matches = (flat_ids[:, None] == jnp.arange(expert_count, dtype=jnp.int32)[None, :]).astype(
        jnp.int32
    )
    earlier = jnp.cumsum(matches, axis=0) - matches
    slot_index = jnp.sum(earlier * matches, axis=1)
    slot_ids = jnp.arange(capacity, dtype=jnp.int32)
    group_rel = (ep_index + jnp.arange(ep_count, dtype=jnp.int32)) % ep_count
    slot_rel = (ctx_index + jnp.arange(ctx_count, dtype=jnp.int32)) % ctx_count
    expert_of = group_rel[:, None] * EXP_DEV + (slot_rel // copies)[None, :]
    routed = (flat_ids[None, None, None, :] == expert_of[:, :, None, None]) & (
        slot_index[None, None, None, :] == slot_ids[None, None, :, None]
    )
    pair_ids = jnp.arange(2, dtype=jnp.int32)
    choose = (pair_ids[None, :, None, None, None, None] == pair_ids[None, None, None, None, :, None]) & (
        routed[:, None, :, :, None, :]
    )
    choose = choose.reshape(ep_count * 2 * ctx_count * capacity, 2 * route_count)
    normed_rep = jnp.repeat(normed, topk_count, axis=0)
    upstream_rep = jnp.repeat(upstream_grad, topk_count, axis=0).astype(jnp.float32)
    scaled_grads = (route_gates.reshape(route_count, 1) * upstream_rep).astype(jnp.bfloat16)
    send_all = jnp.dot(
        choose.astype(jnp.bfloat16),
        jnp.concatenate([normed_rep, scaled_grads]),
        preferred_element_type=jnp.float32,
    ).astype(jnp.bfloat16)
    ep_rows = 2 * ctx_count * capacity
    recv_ep = [send_all[d * ep_rows : (d + 1) * ep_rows] for d in range(ep_count)]
    recv_ep = [recv_ep[0]] + [shifted(recv_ep[d], "ep", d) for d in range(1, ep_count)]
    regrouped = reorder_rows(
        recv_ep, (ep_count, 2, ctx_count, capacity), (2, 1, 0, 3)
    )
    ctx_rows = 2 * ep_count * capacity
    recv_ctx = [regrouped[p * ctx_rows : (p + 1) * ctx_rows] for p in range(ctx_count)]
    recv_ctx = [recv_ctx[0]] + [shifted(recv_ctx[p], "ctx", p) for p in range(1, ctx_count)]
    half = ep_count * capacity
    token_rows = jnp.concatenate([blk[:half] for blk in recv_ctx])
    grad_rows = jnp.concatenate([blk[half:] for blk in recv_ctx])
    partial_value, row_grads = expert_pass(
        token_rows, grad_rows, w_gate[0, 0], w_up[0, 0], w_down[0, 0]
    )
    back_ctx = [partial_value[p * half : (p + 1) * half] for p in range(ctx_count)]
    back_ctx = [back_ctx[0]] + [shifted(back_ctx[p], "ctx", -p) for p in range(1, ctx_count)]
    back_ep = reorder_rows(
        back_ctx, (ctx_count, ep_count, capacity), (1, 0, 2), ep_count
    )
    back_ep = [back_ep[0]] + [shifted(back_ep[d], "ep", -d) for d in range(1, ep_count)]
    held = lax.optimization_barrier((token_rows, grad_rows, row_grads, back_ep))
    gate_total, up_total, down_total = weight_grads(held[0], held[1], *held[2])
    back_ep = held[3]
    to_token = jnp.sum(
        routed.reshape(ep_count, ctx_count * capacity, tok_dev, topk_count), axis=3
    ).astype(jnp.bfloat16)
    d_normed = sum(
        lax.dot_general(
            to_token[d], back_ep[d], (((0,), (0,)), ((), ())), preferred_element_type=jnp.float32
        )
        for d in range(ep_count)
    )
    scaled_norm = norm_gain[None, :] * d_normed
    projection = jnp.mean(state * scaled_norm, axis=1, keepdims=True)
    grad_state = (
        upstream_grad.astype(jnp.float32)
        + inv_rms * scaled_norm
        - state * inv_rms * inv_rms * inv_rms * projection
    ).astype(jnp.bfloat16)
    state_rel = jnp.stack(gather_rel(grad_state, "ep"))
    state_block = jnp.take(
        state_rel, (ep_index - jnp.arange(ep_count, dtype=jnp.int32)) % ep_count, axis=0
    ).reshape(-1, model_width)
    dout = lax.dot_general(
        state_block, out_proj, (((1,), (1,)), ((), ())), preferred_element_type=jnp.float32
    ).astype(jnp.bfloat16)
    dout_own = dout.reshape(tok_ctx, head_count, HD)
    row_delta = jnp.einsum(
        "qhd,hqd->hq", dout_own.astype(jnp.float32), attn_out, precision=PRECISE
    )

    prob_grad = jnp.einsum("qhd,khd->hqk", dout_own, v_all, preferred_element_type=jnp.float32)
    score_grad = (probs * (prob_grad - row_delta[:, :, None])).astype(jnp.bfloat16)
    query_grad = (
        jnp.einsum("hqk,khd->qhd", score_grad, k_all, preferred_element_type=jnp.float32) * scale
    )

    dout_rel = gather_rel(dout, "ctx")
    stats_rel = gather_rel(jnp.stack([log_total, row_delta]), "ctx")
    dout_all = jnp.concatenate(dout_rel).reshape(-1, head_count, HD)
    log_all = jnp.concatenate([s[0] for s in stats_rel], axis=1)
    delta_all = jnp.concatenate([s[1] for s in stats_rel], axis=1)
    key_scores = jnp.einsum("qhd,khd->hqk", q_all, k_own, preferred_element_type=jnp.float32) * scale
    key_allowed = (rel_pos[:, None] >= own_pos[None, :])[None]
    key_probs = jnp.where(key_allowed, jnp.exp(key_scores - log_all[:, :, None]), 0.0)
    value_grad = jnp.einsum(
        "hqk,qhd->khd", key_probs.astype(jnp.bfloat16), dout_all, preferred_element_type=jnp.float32
    )
    key_prob_grad = jnp.einsum(
        "qhd,khd->hqk", dout_all, v_own, preferred_element_type=jnp.float32
    )
    key_score_grad = (key_probs * (key_prob_grad - delta_all[:, :, None])).astype(jnp.bfloat16)
    key_grad = (
        jnp.einsum("hqk,qhd->khd", key_score_grad, q_all, preferred_element_type=jnp.float32)
        * scale
    )
    flat_width = head_count * HD
    return (
        grad_state,
        query_grad.reshape(tok_ctx, flat_width).astype(jnp.bfloat16),
        key_grad.reshape(tok_ctx, flat_width).astype(jnp.bfloat16),
        value_grad.reshape(tok_ctx, flat_width).astype(jnp.bfloat16),
        gate_total.astype(jnp.bfloat16)[None, None],
        up_total.astype(jnp.bfloat16)[None, None],
        down_total.astype(jnp.bfloat16)[None, None],
    )


def solution(mesh):
    placed = (
        P(("ctx", "ep"), None),
        P(("ctx", "ep"), None),
        P(("ctx", "ep"), None),
        P(("ctx", "ep"), None),
        P(),
        P("ep", "ctx", None, None),
        P("ep", "ctx", None, None),
        P("ep", "ctx", None, None),
        P("ep", None),
        P("ctx", "ep"),
        P("ctx", "ep"),
        P("ctx", "ep"),
    )
    return jax.shard_map(
        local,
        mesh=mesh,
        in_specs=placed,
        out_specs=(
            P(("ctx", "ep"), None),
            P("ctx", "ep"),
            P("ctx", "ep"),
            P("ctx", "ep"),
            P("ep", "ctx", None, None),
            P("ep", "ctx", None, None),
            P("ep", "ctx", None, None),
        ),
        check_vma=False,
    )
```

```python
import math

import jax
import numpy as np
import jax.numpy as jnp
from jax import lax
from jax.sharding import PartitionSpec as P

HD = 128
EXP_DEV = 4


EPSILON = 1e-06
FLOOR_SCORE = -1e30
PRECISE = lax.Precision.HIGHEST


def shifted(block, axis, distance):
    devices = range(lax.axis_size(axis))
    route = [((i - distance) % len(devices), i) for i in devices]
    return lax.ppermute(block, axis, route)


def expert_pass(token_rows, grad_rows, gate_rows, up_rows, down_rows):
    contract = (((1,), (1,)), ((), ()))
    pre_gate = lax.dot_general(token_rows, gate_rows, contract, preferred_element_type=jnp.float32)
    up_value = lax.dot_general(token_rows, up_rows, contract, preferred_element_type=jnp.float32)
    sigmoid = jax.nn.sigmoid(pre_gate)
    activation = (pre_gate * sigmoid * up_value).astype(jnp.bfloat16)
    act_grad = lax.dot_general(grad_rows, down_rows, contract, preferred_element_type=jnp.float32)
    up_grad = (act_grad * pre_gate * sigmoid).astype(jnp.bfloat16)
    gate_grad = (act_grad * up_value * sigmoid * (1.0 + pre_gate * (1.0 - sigmoid))).astype(
        jnp.bfloat16
    )
    partial_value = (
        jnp.dot(gate_grad, gate_rows, preferred_element_type=jnp.float32)
        + jnp.dot(up_grad, up_rows, preferred_element_type=jnp.float32)
    ).astype(jnp.bfloat16)
    return (partial_value, (gate_grad, up_grad, activation))


def weight_grads(token_rows, grad_rows, gate_grad, up_grad, activation):
    over_rows = (((0,), (0,)), ((), ()))
    gate_total = lax.dot_general(
        gate_grad, token_rows, over_rows, preferred_element_type=jnp.float32
    )
    up_total = lax.dot_general(up_grad, token_rows, over_rows, preferred_element_type=jnp.float32)
    down_total = lax.dot_general(
        activation, grad_rows, over_rows, preferred_element_type=jnp.float32
    )
    return (gate_total, up_total, down_total)


def reorder_rows(blocks, dims, order, chunks=1):
    count = int(np.prod(dims))
    source = np.transpose(np.arange(count).reshape(dims), order).reshape(-1)
    pick = (jnp.asarray(source, jnp.int32)[:, None] == jnp.arange(count, dtype=jnp.int32)[None, :])
    pick = pick.astype(blocks[0].dtype)
    size = count // chunks
    if count * blocks[0].shape[1] * 4 * len(blocks) > (32 << 20):
        blocks = [jnp.concatenate(blocks)]
    width = count // len(blocks)
    out = []
    for i in range(chunks):
        total = None
        for k, blk in enumerate(blocks):
            part = jnp.dot(
                pick[i * size : (i + 1) * size, k * width : (k + 1) * width],
                blk,
                preferred_element_type=jnp.float32,
            )
            total = part if total is None else total + part
        out.append(total.astype(blocks[0].dtype))
    return out[0] if chunks == 1 else out


def gather_rel(block, axis):
    count = lax.axis_size(axis)
    return [block] + [shifted(block, axis, d) for d in range(1, count)]


def gather_abs(block, axis):
    count = lax.axis_size(axis)
    index = lax.axis_index(axis)
    if count % 2:
        ordered = jnp.stack(gather_rel(block, axis))
        return jnp.take(ordered, (index - jnp.arange(count)) % count, axis=0)
    partner = lax.ppermute(block, axis, [(i, i ^ 1) for i in range(count)])
    low = index % 2 == 0
    pair = jnp.stack([jnp.where(low, block, partner), jnp.where(low, partner, block)])
    groups = count // 2
    if groups == 1:
        return pair
    arrived = [pair] + [
        lax.ppermute(pair, axis, [(i, (i + 2 * d) % count) for i in range(count)])
        for d in range(1, groups)
    ]
    ordered = jnp.take(
        jnp.stack(arrived), (index // 2 - jnp.arange(groups)) % groups, axis=0
    )
    return ordered.reshape((count,) + block.shape)


def local(
    hidden_state,
    upstream_grad,
    route_ids,
    route_gates,
    norm_gain,
    w_gate,
    w_up,
    w_down,
    out_proj,
    queries,
    key_rows,
    value_rows,
):
    ep_count = lax.axis_size("ep")
    ctx_count = lax.axis_size("ctx")
    tok_dev, model_width = hidden_state.shape
    topk_count = route_ids.shape[1]
    expert_count = EXP_DEV * ep_count
    copies = ctx_count // EXP_DEV
    capacity = max(2, 2 * tok_dev * topk_count // expert_count)
    route_count = tok_dev * topk_count
    tok_ctx = queries.shape[0]
    head_count = queries.shape[1] // HD
    ctx_index = lax.axis_index("ctx")
    ep_index = lax.axis_index("ep")
    scale = 1.0 / math.sqrt(HD)

    qkv_all = gather_abs(jnp.stack([queries, key_rows, value_rows]), "ctx")
    block_pos = jnp.arange(tok_ctx, dtype=jnp.int32)
    rel_pos = jnp.arange(ctx_count * tok_ctx, dtype=jnp.int32)
    own_pos = ctx_index * tok_ctx + block_pos
    q_all = qkv_all[:, 0].reshape(-1, head_count, HD)
    k_all = qkv_all[:, 1].reshape(-1, head_count, HD)
    v_all = qkv_all[:, 2].reshape(-1, head_count, HD)
    q_own = queries.reshape(tok_ctx, head_count, HD)
    k_own = key_rows.reshape(tok_ctx, head_count, HD)
    v_own = value_rows.reshape(tok_ctx, head_count, HD)

    raw_scores = jnp.einsum("qhd,khd->hqk", q_own, k_all, preferred_element_type=jnp.float32) * scale
    allowed = (own_pos[:, None] >= rel_pos[None, :])[None]
    row_top = jnp.max(jnp.where(allowed, raw_scores, FLOOR_SCORE), axis=2)
    row_total = jnp.sum(jnp.where(allowed, jnp.exp(raw_scores - row_top[:, :, None]), 0.0), axis=2)
    log_total = row_top + jnp.log(row_total)
    probs = jnp.where(allowed, jnp.exp(raw_scores - log_total[:, :, None]), 0.0)
    attn_out = jnp.einsum("hqk,khd->hqd", probs, v_all.astype(jnp.float32), precision=PRECISE)

    state = hidden_state.astype(jnp.float32)
    inv_rms = lax.rsqrt(jnp.mean(state * state, axis=1, keepdims=True) + EPSILON)
    normed = (state * inv_rms * norm_gain[None, :]).astype(jnp.bfloat16)
    flat_ids = route_ids.reshape(route_count)
    matches = (flat_ids[:, None] == jnp.arange(expert_count, dtype=jnp.int32)[None, :]).astype(
        jnp.int32
    )
    earlier = jnp.cumsum(matches, axis=0) - matches
    slot_index = jnp.sum(earlier * matches, axis=1)
    slot_ids = jnp.arange(capacity, dtype=jnp.int32)
    group_rel = (ep_index + jnp.arange(ep_count, dtype=jnp.int32)) % ep_count
    slot_rel = (ctx_index + jnp.arange(ctx_count, dtype=jnp.int32)) % ctx_count
    expert_of = group_rel[:, None] * EXP_DEV + (slot_rel // copies)[None, :]
    routed = (flat_ids[None, None, None, :] == expert_of[:, :, None, None]) & (
        slot_index[None, None, None, :] == slot_ids[None, None, :, None]
    )
    pair_ids = jnp.arange(2, dtype=jnp.int32)
    choose = (pair_ids[None, :, None, None, None, None] == pair_ids[None, None, None, None, :, None]) & (
        routed[:, None, :, :, None, :]
    )
    choose = choose.reshape(ep_count * 2 * ctx_count * capacity, 2 * route_count)
    normed_rep = jnp.repeat(normed, topk_count, axis=0)
    upstream_rep = jnp.repeat(upstream_grad, topk_count, axis=0).astype(jnp.float32)
    scaled_grads = (route_gates.reshape(route_count, 1) * upstream_rep).astype(jnp.bfloat16)
    send_all = jnp.dot(
        choose.astype(jnp.bfloat16),
        jnp.concatenate([normed_rep, scaled_grads]),
        preferred_element_type=jnp.float32,
    ).astype(jnp.bfloat16)
    ep_rows = 2 * ctx_count * capacity
    recv_ep = [send_all[d * ep_rows : (d + 1) * ep_rows] for d in range(ep_count)]
    recv_ep = [recv_ep[0]] + [shifted(recv_ep[d], "ep", d) for d in range(1, ep_count)]
    regrouped = reorder_rows(
        recv_ep, (ep_count, 2, ctx_count, capacity), (2, 1, 0, 3)
    )
    ctx_rows = 2 * ep_count * capacity
    recv_ctx = [regrouped[p * ctx_rows : (p + 1) * ctx_rows] for p in range(ctx_count)]
    recv_ctx = [recv_ctx[0]] + [shifted(recv_ctx[p], "ctx", p) for p in range(1, ctx_count)]
    half = ep_count * capacity
    token_rows = jnp.concatenate([blk[:half] for blk in recv_ctx])
    grad_rows = jnp.concatenate([blk[half:] for blk in recv_ctx])
    partial_value, row_grads = expert_pass(
        token_rows, grad_rows, w_gate[0, 0], w_up[0, 0], w_down[0, 0]
    )
    back_ctx = [partial_value[p * half : (p + 1) * half] for p in range(ctx_count)]
    back_ctx = [back_ctx[0]] + [shifted(back_ctx[p], "ctx", -p) for p in range(1, ctx_count)]
    back_ep = reorder_rows(
        back_ctx, (ctx_count, ep_count, capacity), (1, 0, 2), ep_count
    )
    back_ep = [back_ep[0]] + [shifted(back_ep[d], "ep", -d) for d in range(1, ep_count)]
    held = lax.optimization_barrier((token_rows, grad_rows, row_grads, back_ep))
    gate_total, up_total, down_total = weight_grads(held[0], held[1], *held[2])
    back_ep = held[3]
    to_token = jnp.sum(
        routed.reshape(ep_count, ctx_count * capacity, tok_dev, topk_count), axis=3
    ).astype(jnp.bfloat16)
    d_normed = sum(
        lax.dot_general(
            to_token[d], back_ep[d], (((0,), (0,)), ((), ())), preferred_element_type=jnp.float32
        )
        for d in range(ep_count)
    )
    scaled_norm = norm_gain[None, :] * d_normed
    projection = jnp.mean(state * scaled_norm, axis=1, keepdims=True)
    grad_state = (
        upstream_grad.astype(jnp.float32)
        + inv_rms * scaled_norm
        - state * inv_rms * inv_rms * inv_rms * projection
    ).astype(jnp.bfloat16)
    state_block = gather_abs(grad_state, "ep").reshape(-1, model_width)
    dout = lax.dot_general(
        state_block, out_proj, (((1,), (1,)), ((), ())), preferred_element_type=jnp.float32
    ).astype(jnp.bfloat16)
    dout_own = dout.reshape(tok_ctx, head_count, HD)
    row_delta = jnp.einsum(
        "qhd,hqd->hq", dout_own.astype(jnp.float32), attn_out, precision=PRECISE
    )

    prob_grad = jnp.einsum("qhd,khd->hqk", dout_own, v_all, preferred_element_type=jnp.float32)
    score_grad = (probs * (prob_grad - row_delta[:, :, None])).astype(jnp.bfloat16)
    query_grad = (
        jnp.einsum("hqk,khd->qhd", score_grad, k_all, preferred_element_type=jnp.float32) * scale
    )

    dout_all = gather_abs(dout, "ctx").reshape(-1, head_count, HD)
    stats_all = gather_abs(jnp.stack([log_total, row_delta]), "ctx")
    log_all = jnp.concatenate([blk[0] for blk in stats_all], axis=1)
    delta_all = jnp.concatenate([blk[1] for blk in stats_all], axis=1)
    key_scores = jnp.einsum("qhd,khd->hqk", q_all, k_own, preferred_element_type=jnp.float32) * scale
    key_allowed = (rel_pos[:, None] >= own_pos[None, :])[None]
    key_probs = jnp.where(key_allowed, jnp.exp(key_scores - log_all[:, :, None]), 0.0)
    value_grad = jnp.einsum(
        "hqk,qhd->khd", key_probs.astype(jnp.bfloat16), dout_all, preferred_element_type=jnp.float32
    )
    key_prob_grad = jnp.einsum(
        "qhd,khd->hqk", dout_all, v_own, preferred_element_type=jnp.float32
    )
    key_score_grad = (key_probs * (key_prob_grad - delta_all[:, :, None])).astype(jnp.bfloat16)
    key_grad = (
        jnp.einsum("hqk,qhd->khd", key_score_grad, q_all, preferred_element_type=jnp.float32)
        * scale
    )
    flat_width = head_count * HD
    return (
        grad_state,
        query_grad.reshape(tok_ctx, flat_width).astype(jnp.bfloat16),
        key_grad.reshape(tok_ctx, flat_width).astype(jnp.bfloat16),
        value_grad.reshape(tok_ctx, flat_width).astype(jnp.bfloat16),
        gate_total.astype(jnp.bfloat16)[None, None],
        up_total.astype(jnp.bfloat16)[None, None],
        down_total.astype(jnp.bfloat16)[None, None],
    )


def solution(mesh):
    placed = (
        P(("ctx", "ep"), None),
        P(("ctx", "ep"), None),
        P(("ctx", "ep"), None),
        P(("ctx", "ep"), None),
        P(),
        P("ep", "ctx", None, None),
        P("ep", "ctx", None, None),
        P("ep", "ctx", None, None),
        P("ep", None),
        P("ctx", "ep"),
        P("ctx", "ep"),
        P("ctx", "ep"),
    )
    return jax.shard_map(
        local,
        mesh=mesh,
        in_specs=placed,
        out_specs=(
            P(("ctx", "ep"), None),
            P("ctx", "ep"),
            P("ctx", "ep"),
            P("ctx", "ep"),
            P("ep", "ctx", None, None),
            P("ep", "ctx", None, None),
            P("ep", "ctx", None, None),
        ),
        check_vma=False,
    )
```

```python
import math

import jax
import numpy as np
import jax.numpy as jnp
from jax import lax
from jax.sharding import PartitionSpec as P

HD = 128
EXP_DEV = 4


EPSILON = 1e-06
FLOOR_SCORE = -1e30
PRECISE = lax.Precision.HIGHEST


def shifted(block, axis, distance):
    devices = range(lax.axis_size(axis))
    route = [((i - distance) % len(devices), i) for i in devices]
    return lax.ppermute(block, axis, route)


def expert_pass(token_rows, grad_rows, gate_rows, up_rows, down_rows):
    contract = (((1,), (1,)), ((), ()))
    pre_gate = lax.dot_general(token_rows, gate_rows, contract, preferred_element_type=jnp.float32)
    up_value = lax.dot_general(token_rows, up_rows, contract, preferred_element_type=jnp.float32)
    sigmoid = jax.nn.sigmoid(pre_gate)
    activation = (pre_gate * sigmoid * up_value).astype(jnp.bfloat16)
    act_grad = lax.dot_general(grad_rows, down_rows, contract, preferred_element_type=jnp.float32)
    up_grad = (act_grad * pre_gate * sigmoid).astype(jnp.bfloat16)
    gate_grad = (act_grad * up_value * sigmoid * (1.0 + pre_gate * (1.0 - sigmoid))).astype(
        jnp.bfloat16
    )
    partial_value = (
        jnp.dot(gate_grad, gate_rows, preferred_element_type=jnp.float32)
        + jnp.dot(up_grad, up_rows, preferred_element_type=jnp.float32)
    ).astype(jnp.bfloat16)
    return (partial_value, (gate_grad, up_grad, activation))


def reorder_rows(blocks, dims, order, chunks=1):
    count = int(np.prod(dims))
    source = np.transpose(np.arange(count).reshape(dims), order).reshape(-1)
    pick = (jnp.asarray(source, jnp.int32)[:, None] == jnp.arange(count, dtype=jnp.int32)[None, :])
    pick = pick.astype(blocks[0].dtype)
    size = count // chunks
    if count * blocks[0].shape[1] * 4 * len(blocks) > (32 << 20):
        blocks = [jnp.concatenate(blocks)]
    width = count // len(blocks)
    out = []
    for i in range(chunks):
        total = None
        for k, blk in enumerate(blocks):
            part = jnp.dot(
                pick[i * size : (i + 1) * size, k * width : (k + 1) * width],
                blk,
                preferred_element_type=jnp.float32,
            )
            total = part if total is None else total + part
        out.append(total.astype(blocks[0].dtype))
    return out[0] if chunks == 1 else out


def gather_rel(block, axis):
    count = lax.axis_size(axis)
    return [block] + [shifted(block, axis, d) for d in range(1, count)]


def gather_abs(block, axis):
    count = lax.axis_size(axis)
    index = lax.axis_index(axis)
    if count % 2:
        ordered = jnp.stack(gather_rel(block, axis))
        return jnp.take(ordered, (index - jnp.arange(count)) % count, axis=0)
    partner = lax.ppermute(block, axis, [(i, i ^ 1) for i in range(count)])
    low = index % 2 == 0
    pair = jnp.stack([jnp.where(low, block, partner), jnp.where(low, partner, block)])
    groups = count // 2
    if groups == 1:
        return pair
    arrived = [pair] + [
        lax.ppermute(pair, axis, [(i, (i + 2 * d) % count) for i in range(count)])
        for d in range(1, groups)
    ]
    ordered = jnp.take(
        jnp.stack(arrived), (index // 2 - jnp.arange(groups)) % groups, axis=0
    )
    return ordered.reshape((count,) + block.shape)


def local(
    hidden_state,
    upstream_grad,
    route_ids,
    route_gates,
    norm_gain,
    w_gate,
    w_up,
    w_down,
    out_proj,
    queries,
    key_rows,
    value_rows,
):
    ep_count = lax.axis_size("ep")
    ctx_count = lax.axis_size("ctx")
    tok_dev, model_width = hidden_state.shape
    topk_count = route_ids.shape[1]
    expert_count = EXP_DEV * ep_count
    copies = ctx_count // EXP_DEV
    capacity = max(2, 2 * tok_dev * topk_count // expert_count)
    route_count = tok_dev * topk_count
    tok_ctx = queries.shape[0]
    head_count = queries.shape[1] // HD
    ctx_index = lax.axis_index("ctx")
    ep_index = lax.axis_index("ep")
    scale = 1.0 / math.sqrt(HD)

    qkv_all = gather_abs(jnp.stack([queries, key_rows, value_rows]), "ctx")
    block_pos = jnp.arange(tok_ctx, dtype=jnp.int32)
    rel_pos = jnp.arange(ctx_count * tok_ctx, dtype=jnp.int32)
    own_pos = ctx_index * tok_ctx + block_pos
    q_all = qkv_all[:, 0].reshape(-1, head_count, HD)
    k_all = qkv_all[:, 1].reshape(-1, head_count, HD)
    v_all = qkv_all[:, 2].reshape(-1, head_count, HD)
    q_own = queries.reshape(tok_ctx, head_count, HD)
    k_own = key_rows.reshape(tok_ctx, head_count, HD)
    v_own = value_rows.reshape(tok_ctx, head_count, HD)

    raw_scores = jnp.einsum("qhd,khd->hqk", q_own, k_all, preferred_element_type=jnp.float32) * scale
    allowed = (own_pos[:, None] >= rel_pos[None, :])[None]
    row_top = jnp.max(jnp.where(allowed, raw_scores, FLOOR_SCORE), axis=2)
    row_total = jnp.sum(jnp.where(allowed, jnp.exp(raw_scores - row_top[:, :, None]), 0.0), axis=2)
    log_total = row_top + jnp.log(row_total)
    probs = jnp.where(allowed, jnp.exp(raw_scores - log_total[:, :, None]), 0.0)
    attn_out = jnp.einsum("hqk,khd->hqd", probs, v_all.astype(jnp.float32), precision=PRECISE)

    state = hidden_state.astype(jnp.float32)
    inv_rms = lax.rsqrt(jnp.mean(state * state, axis=1, keepdims=True) + EPSILON)
    normed = (state * inv_rms * norm_gain[None, :]).astype(jnp.bfloat16)
    flat_ids = route_ids.reshape(route_count)
    matches = (flat_ids[:, None] == jnp.arange(expert_count, dtype=jnp.int32)[None, :]).astype(
        jnp.int32
    )
    earlier = jnp.cumsum(matches, axis=0) - matches
    slot_index = jnp.sum(earlier * matches, axis=1)
    slot_ids = jnp.arange(capacity, dtype=jnp.int32)
    group_rel = (ep_index + jnp.arange(ep_count, dtype=jnp.int32)) % ep_count
    slot_rel = (ctx_index + jnp.arange(ctx_count, dtype=jnp.int32)) % ctx_count
    expert_of = group_rel[:, None] * EXP_DEV + (slot_rel // copies)[None, :]
    routed = (flat_ids[None, None, None, :] == expert_of[:, :, None, None]) & (
        slot_index[None, None, None, :] == slot_ids[None, None, :, None]
    )
    pair_ids = jnp.arange(2, dtype=jnp.int32)
    choose = (pair_ids[None, :, None, None, None, None] == pair_ids[None, None, None, None, :, None]) & (
        routed[:, None, :, :, None, :]
    )
    choose = choose.reshape(ep_count * 2 * ctx_count * capacity, 2 * route_count)
    normed_rep = jnp.repeat(normed, topk_count, axis=0)
    upstream_rep = jnp.repeat(upstream_grad, topk_count, axis=0).astype(jnp.float32)
    scaled_grads = (route_gates.reshape(route_count, 1) * upstream_rep).astype(jnp.bfloat16)
    send_all = jnp.dot(
        choose.astype(jnp.bfloat16),
        jnp.concatenate([normed_rep, scaled_grads]),
        preferred_element_type=jnp.float32,
    ).astype(jnp.bfloat16)
    ep_rows = 2 * ctx_count * capacity
    recv_ep = [send_all[d * ep_rows : (d + 1) * ep_rows] for d in range(ep_count)]
    recv_ep = [recv_ep[0]] + [shifted(recv_ep[d], "ep", d) for d in range(1, ep_count)]
    regrouped = reorder_rows(
        recv_ep, (ep_count, 2, ctx_count, capacity), (2, 1, 0, 3)
    )
    ctx_rows = 2 * ep_count * capacity
    recv_ctx = [regrouped[p * ctx_rows : (p + 1) * ctx_rows] for p in range(ctx_count)]
    recv_ctx = [recv_ctx[0]] + [shifted(recv_ctx[p], "ctx", p) for p in range(1, ctx_count)]
    half = ep_count * capacity
    token_rows = jnp.concatenate([blk[:half] for blk in recv_ctx])
    grad_rows = jnp.concatenate([blk[half:] for blk in recv_ctx])
    partial_value, row_grads = expert_pass(
        token_rows, grad_rows, w_gate[0, 0], w_up[0, 0], w_down[0, 0]
    )
    back_ctx = [partial_value[p * half : (p + 1) * half] for p in range(ctx_count)]
    back_ctx = [back_ctx[0]] + [
        shifted(back_ctx[p], "ctx", -p) for p in range(1, ctx_count)
    ]
    down_total = lax.dot_general(
        row_grads[2], grad_rows, (((0,), (0,)), ((), ())), preferred_element_type=jnp.float32
    )
    back_ep = reorder_rows(
        back_ctx, (ctx_count, ep_count, capacity), (1, 0, 2), ep_count
    )
    back_ep = [back_ep[0]] + [shifted(back_ep[d], "ep", -d) for d in range(1, ep_count)]
    held = lax.optimization_barrier((token_rows, row_grads[0], row_grads[1], back_ep))
    over_rows = (((0,), (0,)), ((), ()))
    gate_total = lax.dot_general(held[1], held[0], over_rows, preferred_element_type=jnp.float32)
    up_total = lax.dot_general(held[2], held[0], over_rows, preferred_element_type=jnp.float32)
    back_ep = held[3]
    to_token = jnp.sum(
        routed.reshape(ep_count, ctx_count * capacity, tok_dev, topk_count), axis=3
    ).astype(jnp.bfloat16)
    d_normed = sum(
        lax.dot_general(
            to_token[d], back_ep[d], (((0,), (0,)), ((), ())), preferred_element_type=jnp.float32
        )
        for d in range(ep_count)
    )
    scaled_norm = norm_gain[None, :] * d_normed
    projection = jnp.mean(state * scaled_norm, axis=1, keepdims=True)
    grad_state = (
        upstream_grad.astype(jnp.float32)
        + inv_rms * scaled_norm
        - state * inv_rms * inv_rms * inv_rms * projection
    ).astype(jnp.bfloat16)
    state_block = gather_abs(grad_state, "ep").reshape(-1, model_width)
    dout = lax.dot_general(
        state_block, out_proj, (((1,), (1,)), ((), ())), preferred_element_type=jnp.float32
    ).astype(jnp.bfloat16)
    dout_own = dout.reshape(tok_ctx, head_count, HD)
    row_delta = jnp.einsum(
        "qhd,hqd->hq", dout_own.astype(jnp.float32), attn_out, precision=PRECISE
    )

    prob_grad = jnp.einsum("qhd,khd->hqk", dout_own, v_all, preferred_element_type=jnp.float32)
    score_grad = (probs * (prob_grad - row_delta[:, :, None])).astype(jnp.bfloat16)
    query_grad = (
        jnp.einsum("hqk,khd->qhd", score_grad, k_all, preferred_element_type=jnp.float32) * scale
    )

    dout_all = gather_abs(dout, "ctx").reshape(-1, head_count, HD)
    stats_all = gather_abs(jnp.stack([log_total, row_delta]), "ctx")
    log_all = jnp.concatenate([blk[0] for blk in stats_all], axis=1)
    delta_all = jnp.concatenate([blk[1] for blk in stats_all], axis=1)
    key_scores = jnp.einsum("qhd,khd->hqk", q_all, k_own, preferred_element_type=jnp.float32) * scale
    key_allowed = (rel_pos[:, None] >= own_pos[None, :])[None]
    key_probs = jnp.where(key_allowed, jnp.exp(key_scores - log_all[:, :, None]), 0.0)
    value_grad = jnp.einsum(
        "hqk,qhd->khd", key_probs.astype(jnp.bfloat16), dout_all, preferred_element_type=jnp.float32
    )
    key_prob_grad = jnp.einsum(
        "qhd,khd->hqk", dout_all, v_own, preferred_element_type=jnp.float32
    )
    key_score_grad = (key_probs * (key_prob_grad - delta_all[:, :, None])).astype(jnp.bfloat16)
    key_grad = (
        jnp.einsum("hqk,qhd->khd", key_score_grad, q_all, preferred_element_type=jnp.float32)
        * scale
    )
    flat_width = head_count * HD
    return (
        grad_state,
        query_grad.reshape(tok_ctx, flat_width).astype(jnp.bfloat16),
        key_grad.reshape(tok_ctx, flat_width).astype(jnp.bfloat16),
        value_grad.reshape(tok_ctx, flat_width).astype(jnp.bfloat16),
        gate_total.astype(jnp.bfloat16)[None, None],
        up_total.astype(jnp.bfloat16)[None, None],
        down_total.astype(jnp.bfloat16)[None, None],
    )


def solution(mesh):
    placed = (
        P(("ctx", "ep"), None),
        P(("ctx", "ep"), None),
        P(("ctx", "ep"), None),
        P(("ctx", "ep"), None),
        P(),
        P("ep", "ctx", None, None),
        P("ep", "ctx", None, None),
        P("ep", "ctx", None, None),
        P("ep", None),
        P("ctx", "ep"),
        P("ctx", "ep"),
        P("ctx", "ep"),
    )

    return jax.shard_map(
        local,
        mesh=mesh,
        in_specs=placed,
        out_specs=(
            P(("ctx", "ep"), None),
            P("ctx", "ep"),
            P("ctx", "ep"),
            P("ctx", "ep"),
            P("ep", "ctx", None, None),
            P("ep", "ctx", None, None),
            P("ep", "ctx", None, None),
        ),
        check_vma=False,
    )
```
